32 devices in a mesh: occ: 4 (over z), aux: 4 (over x, core), vir: 2 (over y).
Axes of the slice: x: 2, y: 2, z: 4, core: 2. Of those that a mesh axis runs over, the one named last changes fastest.
Arguments:
- integrals: bfloat16 [4, 2048, 4096], P('occ', 'vir', 'aux'), may hold values from -0.65625 to 0.65625
- occ_energy: float32 [4], replicated, may hold values from -2 to -0.5
- vir_energy: float32 [2048], replicated, may hold values from 0.25 to 3
Outputs:
- lagrangian: bfloat16 [4, 2048, 4096], P('occ', 'vir', 'aux')
The draws below stay inside these ranges and needn't reach their ends.
All inputs are finite; a program needn't handle non-finite values.
Results may differ from the reference program's by a relative error of at most 0.0039.
Values may be sent and summed in bfloat16 or wider, within the bound.
No kernel may reach another device: no remote copies, remote signals or barrier semaphores. Data moves between devices by JAX's collectives and lax.ppermute only.
A program may use at most 64 MiB of HBM per device.

```python
import jax
import jax.numpy as jnp
from jax import lax

V = 2048
NAUX = 4096
OCC_DEV = 1
NOCC = 4


def shard_levels(own_key, shape, cuts, least, high):
    def one(axis_at, blocks):
        steps = jax.random.uniform(jax.random.fold_in(jax.random.fold_in(own_key, 6), axis_at), (blocks,), jnp.float32, least / len(cuts), high / len(cuts))
        return jnp.repeat(jnp.exp(steps), shape[axis_at] // blocks).reshape((-1,) + (1,) * (len(shape) - axis_at - 1))

    factor_of = one(*cuts[0])
    for cut in cuts[1:]:
        factor_of = factor_of * one(*cut)
    return factor_of


def noise(rng, shape, scale, most, pieces=(), kind=jnp.bfloat16):
    array = scale * jax.random.normal(rng, shape, jnp.float32)
    if pieces:
        array = array * shard_levels(rng, shape, pieces, -0.22, 0.18)
    return jnp.clip(array, -most, most).astype(kind)


def setup_inputs(seed: int = 0) -> dict:
    seeds = jax.random.split(jax.random.key(seed), 4)
    return {
        "integrals": noise(seeds[0], (NOCC, V, NAUX), 0.11, 0.65625, ((0, 4), (1, 2), (2, 4))),
        "occ_energy": jnp.clip(jax.random.uniform(seeds[1], (NOCC,), jnp.float32, -2.0, -0.5), -2.0, -0.5),
        "vir_energy": jnp.clip(jax.random.uniform(seeds[2], (V,), jnp.float32, 0.25, 3.0), 0.25, 3.0),
    }


def pair_block(own_rows, partner_rows, own_level, partner_level, vir_energy):
    pair_values = jnp.dot(own_rows, partner_rows.T, preferred_element_type=jnp.float32)
    denominator = own_level + partner_level - vir_energy[:, None] - vir_energy[None, :]
    amplitudes = (pair_values / denominator).astype(jnp.bfloat16)
    own_part = jnp.dot(amplitudes, partner_rows, preferred_element_type=jnp.float32)
    back_part = jnp.dot(amplitudes.T, own_rows, preferred_element_type=jnp.float32)
    return own_part, back_part


def reference(integrals, occ_energy, vir_energy):
    distance = 2 * OCC_DEV
    partner = jnp.roll(integrals, distance, axis=0)
    partner_energy = jnp.roll(occ_energy, distance)

    def one_pair(inputs):
        return pair_block(inputs[0], inputs[1], inputs[2], inputs[3], vir_energy)

    own_part, back_part = lax.map(one_pair, (integrals, partner, occ_energy, partner_energy))
    back_rows = jnp.roll(back_part, -distance, axis=0)
    return (own_part + back_rows).astype(jnp.bfloat16)
```

```python
import jax
import jax.numpy as jnp
from jax import lax
from jax.sharding import PartitionSpec as P

CHUNKS = 4
AUX_BY_PERMUTE = True


def shifted_2(value, axis, by):
    count = lax.axis_size(axis)
    return lax.ppermute(value, axis, [(i, (i + by) % count) for i in range(count)])


def general_plan(integrals, occ_energy, vir_energy):
    row_count = integrals.shape[0]
    vir_width = integrals.shape[1]
    cycle_size = lax.axis_size("occ")
    position = lax.axis_index("occ")
    own_level = lax.dynamic_slice_in_dim(occ_energy, position * row_count, row_count)
    partner_level = lax.dynamic_slice_in_dim(
        occ_energy, (position - 2) % cycle_size * row_count, row_count
    )
    local_vir = lax.dynamic_slice_in_dim(vir_energy, lax.axis_index("vir") * vir_width, vir_width)
    shifted = shifted_2(integrals, "occ", 2)
    partner = lax.all_gather(shifted, "vir", axis=1, tiled=True)
    virtuals = partner.shape[1]
    pair_level = own_level + partner_level
    share_rows = virtuals // lax.axis_size("aux")
    partial_value = lax.psum_scatter(
        jnp.einsum("nbq,naq->bna", partner, integrals, preferred_element_type=jnp.float32),
        "aux",
        scatter_dimension=0,
        tiled=True,
    )
    first_row = lax.axis_index("aux") * share_rows
    vir_rows = lax.dynamic_slice_in_dim(vir_energy, first_row, share_rows)
    amplitudes = (
        partial_value
        / (pair_level[None, :, None] - vir_rows[:, None, None] - local_vir[None, None, :])
    ).astype(jnp.bfloat16)
    portion = lax.all_gather(amplitudes, "aux", axis=0, tiled=True)
    own_part = jnp.einsum("bna,nbq->naq", portion, partner, preferred_element_type=jnp.float32)
    rows_back = jnp.einsum("bna,naq->nbq", portion, integrals, preferred_element_type=jnp.float32)
    owned = lax.psum_scatter(rows_back, "vir", scatter_dimension=1, tiled=True)
    returned = shifted_2(owned, "occ", -2)
    return (own_part + returned).astype(jnp.bfloat16)


def xor_pairs(count, step):
    return [(j, j ^ step) for j in range(count)]


def aux_reduce_scatter(x):
    count = lax.axis_size("aux")
    k = lax.axis_index("aux")
    first = 0
    step = 1
    while step < count:
        half = x.shape[0] // 2
        bit = (k // step) % 2
        keep = lax.dynamic_slice_in_dim(x, bit * half, half, 0)
        send = lax.dynamic_slice_in_dim(x, (1 - bit) * half, half, 0)
        x = keep + lax.ppermute(send, "aux", xor_pairs(count, step))
        first = first + bit * half
        step *= 2
    return x, first


def aux_all_gather(x):
    count = lax.axis_size("aux")
    k = lax.axis_index("aux")
    step = count // 2
    while step >= 1:
        bit = (k // step) % 2
        other = lax.ppermute(x, "aux", xor_pairs(count, step))
        x = jnp.where(bit == 0, jnp.concatenate([x, other]), jnp.concatenate([other, x]))
        step //= 2
    return x


def paired_plan(integrals, occ_energy, vir_energy):
    own = integrals[0]
    vir_rows, _ = own.shape
    cycle_size = lax.axis_size("occ")
    position = lax.axis_index("occ")
    pair_level = occ_energy[position] + occ_energy[(position - 2) % cycle_size]
    vir_pos = lax.axis_index("vir")
    vir_count = lax.axis_size("vir")
    aux_count = lax.axis_size("aux")
    share = vir_rows // aux_count
    width = vir_rows // CHUNKS

    if not AUX_BY_PERMUTE:
        first_row = lax.axis_index("aux") * share

    total = None
    previous = None
    for c in range(CHUNKS):
        piece = own[c * width:(c + 1) * width]
        if previous is not None:
            piece, _ = lax.optimization_barrier((piece, previous))
        arrived = shifted_2(piece, "occ", 2)
        previous = arrived
        if vir_count == 2:
            mate = shifted_2(arrived, "vir", 1)
            block = jnp.concatenate([arrived, mate])
            cols = [vir_pos, 1 - vir_pos]
        else:
            block = lax.all_gather(arrived, "vir", axis=0, tiled=True)
            cols = list(range(vir_count))
        col_level = jnp.concatenate(
            [lax.dynamic_slice_in_dim(vir_energy, w * vir_rows + c * width, width) for w in cols]
        )
        partial = jnp.einsum("aq,bq->ab", own, block, preferred_element_type=jnp.float32)
        if AUX_BY_PERMUTE:
            summed, first = aux_reduce_scatter(partial)
        else:
            summed = lax.psum_scatter(partial, "aux", scatter_dimension=0, tiled=True)
            first = first_row
        row_level = lax.dynamic_slice_in_dim(vir_energy, vir_pos * vir_rows + first, share)
        amplitudes = (summed / (pair_level - row_level[:, None] - col_level[None, :])).astype(
            jnp.bfloat16
        )
        if AUX_BY_PERMUTE:
            rows = aux_all_gather(amplitudes)
        else:
            rows = lax.all_gather(amplitudes, "aux", axis=0, tiled=True)
        term = jnp.dot(rows, block, preferred_element_type=jnp.float32)
        total = term if total is None else total + term
    gamma_own = total
    gamma_back = total
    return (gamma_own + gamma_back).astype(jnp.bfloat16)[None]


def on_device(integrals, occ_energy, vir_energy):
    cycle_size = lax.axis_size("occ")
    if integrals.shape[0] == 1 and 4 % cycle_size == 0 and integrals.shape[1] % (CHUNKS * 8) == 0:
        return paired_plan(integrals, occ_energy, vir_energy)
    return general_plan(integrals, occ_energy, vir_energy)


def solution(mesh):
    placed = (P("occ", "vir", "aux"), P(), P())
    return jax.shard_map(
        on_device, mesh=mesh, in_specs=placed, out_specs=P("occ", "vir", "aux"), check_vma=False
    )
```

```python
import jax
import jax.numpy as jnp
from jax import lax
from jax.sharding import PartitionSpec as P

CHUNKS = 4
AUX_BY_PERMUTE = True


def shifted_2(value, axis, by):
    count = lax.axis_size(axis)
    return lax.ppermute(value, axis, [(i, (i + by) % count) for i in range(count)])


def general_plan(integrals, occ_energy, vir_energy):
    row_count = integrals.shape[0]
    vir_width = integrals.shape[1]
    cycle_size = lax.axis_size("occ")
    position = lax.axis_index("occ")
    own_level = lax.dynamic_slice_in_dim(occ_energy, position * row_count, row_count)
    partner_level = lax.dynamic_slice_in_dim(
        occ_energy, (position - 2) % cycle_size * row_count, row_count
    )
    local_vir = lax.dynamic_slice_in_dim(vir_energy, lax.axis_index("vir") * vir_width, vir_width)
    shifted = shifted_2(integrals, "occ", 2)
    partner = lax.all_gather(shifted, "vir", axis=1, tiled=True)
    virtuals = partner.shape[1]
    pair_level = own_level + partner_level
    share_rows = virtuals // lax.axis_size("aux")
    partial_value = lax.psum_scatter(
        jnp.einsum("nbq,naq->bna", partner, integrals, preferred_element_type=jnp.float32),
        "aux",
        scatter_dimension=0,
        tiled=True,
    )
    first_row = lax.axis_index("aux") * share_rows
    vir_rows = lax.dynamic_slice_in_dim(vir_energy, first_row, share_rows)
    amplitudes = (
        partial_value
        / (pair_level[None, :, None] - vir_rows[:, None, None] - local_vir[None, None, :])
    ).astype(jnp.bfloat16)
    portion = lax.all_gather(amplitudes, "aux", axis=0, tiled=True)
    own_part = jnp.einsum("bna,nbq->naq", portion, partner, preferred_element_type=jnp.float32)
    rows_back = jnp.einsum("bna,naq->nbq", portion, integrals, preferred_element_type=jnp.float32)
    owned = lax.psum_scatter(rows_back, "vir", scatter_dimension=1, tiled=True)
    returned = shifted_2(owned, "occ", -2)
    return (own_part + returned).astype(jnp.bfloat16)


def xor_pairs(count, step):
    return [(j, j ^ step) for j in range(count)]


def aux_reduce_scatter(x):
    count = lax.axis_size("aux")
    k = lax.axis_index("aux")
    first = 0
    step = 1
    while step < count:
        half = x.shape[0] // 2
        bit = (k // step) % 2
        keep = lax.dynamic_slice_in_dim(x, bit * half, half, 0)
        send = lax.dynamic_slice_in_dim(x, (1 - bit) * half, half, 0)
        x = keep + lax.ppermute(send, "aux", xor_pairs(count, step))
        first = first + bit * half
        step *= 2
    return x, first


def aux_all_gather(x):
    count = lax.axis_size("aux")
    k = lax.axis_index("aux")
    step = count // 2
    while step >= 1:
        bit = (k // step) % 2
        other = lax.ppermute(x, "aux", xor_pairs(count, step))
        x = jnp.where(bit == 0, jnp.concatenate([x, other]), jnp.concatenate([other, x]))
        step //= 2
    return x


def paired_plan(integrals, occ_energy, vir_energy):
    own = integrals[0]
    vir_rows, _ = own.shape
    cycle_size = lax.axis_size("occ")
    position = lax.axis_index("occ")
    pair_level = occ_energy[position] + occ_energy[(position - 2) % cycle_size]
    vir_pos = lax.axis_index("vir")
    vir_count = lax.axis_size("vir")
    aux_count = lax.axis_size("aux")
    share = vir_rows // aux_count
    width = vir_rows // CHUNKS
    if not AUX_BY_PERMUTE:
        first_row = lax.axis_index("aux") * share

    def forward(c, arrived):
        if vir_count == 2:
            mate = shifted_2(arrived, "vir", 1)
            block = jnp.concatenate([arrived, mate])
            cols = [vir_pos, 1 - vir_pos]
        else:
            block = lax.all_gather(arrived, "vir", axis=0, tiled=True)
            cols = list(range(vir_count))
        col_level = jnp.concatenate(
            [lax.dynamic_slice_in_dim(vir_energy, w * vir_rows + c * width, width) for w in cols]
        )
        return block, col_level

    def reduce(block):
        partial = jnp.einsum("aq,bq->ab", own, block, preferred_element_type=jnp.float32)
        if AUX_BY_PERMUTE:
            return aux_reduce_scatter(partial)
        return lax.psum_scatter(partial, "aux", scatter_dimension=0, tiled=True), first_row

    def amplitudes_of(summed, first, col_level):
        row_level = lax.dynamic_slice_in_dim(vir_energy, vir_pos * vir_rows + first, share)
        amplitudes = (summed / (pair_level - row_level[:, None] - col_level[None, :])).astype(
            jnp.bfloat16
        )
        if AUX_BY_PERMUTE:
            return aux_all_gather(amplitudes)
        return lax.all_gather(amplitudes, "aux", axis=0, tiled=True)

    arrived = [None] * CHUNKS
    blocks = [None] * CHUNKS
    levels = [None] * CHUNKS
    summed = [None] * CHUNKS
    firsts = [None] * CHUNKS
    gathered = [None] * CHUNKS
    total = None
    for t in range(CHUNKS + 4):
        piece = own[t * width:(t + 1) * width] if t < CHUNKS else None
        if 0 < t < CHUNKS:
            gate = {"piece": piece, "arrived": arrived[t - 1]}
            if t >= 2:
                gate["block"] = blocks[t - 2]
            if t >= 3:
                gate["summed"] = summed[t - 3]
            if t >= 4:
                gate["gathered"] = gathered[t - 4]
            if total is not None:
                gate["total"] = total
            gate = lax.optimization_barrier(gate)
            piece = gate["piece"]
            arrived[t - 1] = gate["arrived"]
            if t >= 2:
                blocks[t - 2] = gate["block"]
            if t >= 3:
                summed[t - 3] = gate["summed"]
            if t >= 4:
                gathered[t - 4] = gate["gathered"]
            if total is not None:
                total = gate["total"]
        if t < CHUNKS:
            arrived[t] = shifted_2(piece, "occ", 2)
        c = t - 1
        if 0 <= c < CHUNKS:
            blocks[c], levels[c] = forward(c, arrived[c])
        c = t - 2
        if 0 <= c < CHUNKS:
            summed[c], firsts[c] = reduce(blocks[c])
        c = t - 3
        if 0 <= c < CHUNKS:
            gathered[c] = amplitudes_of(summed[c], firsts[c], levels[c])
        c = t - 4
        if 0 <= c < CHUNKS:
            term = jnp.dot(gathered[c], blocks[c], preferred_element_type=jnp.float32)
            total = term if total is None else total + term
    gamma_own = total
    gamma_back = total
    return (gamma_own + gamma_back).astype(jnp.bfloat16)[None]


def on_device(integrals, occ_energy, vir_energy):
    cycle_size = lax.axis_size("occ")
    if integrals.shape[0] == 1 and 4 % cycle_size == 0 and integrals.shape[1] % (CHUNKS * 8) == 0:
        return paired_plan(integrals, occ_energy, vir_energy)
    return general_plan(integrals, occ_energy, vir_energy)


def solution(mesh):
    placed = (P("occ", "vir", "aux"), P(), P())
    return jax.shard_map(
        on_device, mesh=mesh, in_specs=placed, out_specs=P("occ", "vir", "aux"), check_vma=False
    )
```

```python
import jax
import jax.numpy as jnp
from jax import lax
from jax.sharding import PartitionSpec as P

CHUNKS = 4
AUX_BY_PERMUTE = True
Z_GATED = False


def shifted_2(value, axis, by):
    count = lax.axis_size(axis)
    return lax.ppermute(value, axis, [(i, (i + by) % count) for i in range(count)])


def general_plan(integrals, occ_energy, vir_energy):
    row_count = integrals.shape[0]
    vir_width = integrals.shape[1]
    cycle_size = lax.axis_size("occ")
    position = lax.axis_index("occ")
    own_level = lax.dynamic_slice_in_dim(occ_energy, position * row_count, row_count)
    partner_level = lax.dynamic_slice_in_dim(
        occ_energy, (position - 2) % cycle_size * row_count, row_count
    )
    local_vir = lax.dynamic_slice_in_dim(vir_energy, lax.axis_index("vir") * vir_width, vir_width)
    shifted = shifted_2(integrals, "occ", 2)
    partner = lax.all_gather(shifted, "vir", axis=1, tiled=True)
    virtuals = partner.shape[1]
    pair_level = own_level + partner_level
    share_rows = virtuals // lax.axis_size("aux")
    partial_value = lax.psum_scatter(
        jnp.einsum("nbq,naq->bna", partner, integrals, preferred_element_type=jnp.float32),
        "aux",
        scatter_dimension=0,
        tiled=True,
    )
    first_row = lax.axis_index("aux") * share_rows
    vir_rows = lax.dynamic_slice_in_dim(vir_energy, first_row, share_rows)
    amplitudes = (
        partial_value
        / (pair_level[None, :, None] - vir_rows[:, None, None] - local_vir[None, None, :])
    ).astype(jnp.bfloat16)
    portion = lax.all_gather(amplitudes, "aux", axis=0, tiled=True)
    own_part = jnp.einsum("bna,nbq->naq", portion, partner, preferred_element_type=jnp.float32)
    rows_back = jnp.einsum("bna,naq->nbq", portion, integrals, preferred_element_type=jnp.float32)
    owned = lax.psum_scatter(rows_back, "vir", scatter_dimension=1, tiled=True)
    returned = shifted_2(owned, "occ", -2)
    return (own_part + returned).astype(jnp.bfloat16)


def xor_pairs(count, step):
    return [(j, j ^ step) for j in range(count)]


def aux_reduce_scatter(x):
    count = lax.axis_size("aux")
    k = lax.axis_index("aux")
    first = 0
    step = 1
    while step < count:
        half = x.shape[0] // 2
        bit = (k // step) % 2
        keep = lax.dynamic_slice_in_dim(x, bit * half, half, 0)
        send = lax.dynamic_slice_in_dim(x, (1 - bit) * half, half, 0)
        x = keep + lax.ppermute(send, "aux", xor_pairs(count, step))
        first = first + bit * half
        step *= 2
    return x, first


def aux_all_gather(x):
    count = lax.axis_size("aux")
    k = lax.axis_index("aux")
    step = count // 2
    while step >= 1:
        bit = (k // step) % 2
        other = lax.ppermute(x, "aux", xor_pairs(count, step))
        x = jnp.where(bit == 0, jnp.concatenate([x, other]), jnp.concatenate([other, x]))
        step //= 2
    return x


def paired_plan(integrals, occ_energy, vir_energy):
    own = integrals[0]
    vir_rows, _ = own.shape
    cycle_size = lax.axis_size("occ")
    position = lax.axis_index("occ")
    pair_level = occ_energy[position] + occ_energy[(position - 2) % cycle_size]
    vir_pos = lax.axis_index("vir")
    vir_count = lax.axis_size("vir")
    aux_count = lax.axis_size("aux")
    share = vir_rows // aux_count
    width = vir_rows // CHUNKS
    if not AUX_BY_PERMUTE:
        first_row = lax.axis_index("aux") * share

    def forward(c, arrived):
        if vir_count == 2:
            mate = shifted_2(arrived, "vir", 1)
            block = jnp.concatenate([arrived, mate])
            cols = [vir_pos, 1 - vir_pos]
        else:
            block = lax.all_gather(arrived, "vir", axis=0, tiled=True)
            cols = list(range(vir_count))
        col_level = jnp.concatenate(
            [lax.dynamic_slice_in_dim(vir_energy, w * vir_rows + c * width, width) for w in cols]
        )
        return block, col_level

    def reduce(block):
        partial = jnp.einsum("aq,bq->ab", own, block, preferred_element_type=jnp.float32)
        if AUX_BY_PERMUTE:
            return aux_reduce_scatter(partial)
        return lax.psum_scatter(partial, "aux", scatter_dimension=0, tiled=True), first_row

    def amplitudes_of(summed, first, col_level):
        row_level = lax.dynamic_slice_in_dim(vir_energy, vir_pos * vir_rows + first, share)
        amplitudes = (summed / (pair_level - row_level[:, None] - col_level[None, :])).astype(
            jnp.bfloat16
        )
        if AUX_BY_PERMUTE:
            return aux_all_gather(amplitudes)
        return lax.all_gather(amplitudes, "aux", axis=0, tiled=True)

    arrived = [None] * CHUNKS
    blocks = [None] * CHUNKS
    levels = [None] * CHUNKS
    summed = [None] * CHUNKS
    firsts = [None] * CHUNKS
    gathered = [None] * CHUNKS
    total = None
    for c in range(CHUNKS if not Z_GATED else 0):
        arrived[c] = shifted_2(own[c * width:(c + 1) * width], "occ", 2)
    for t in range(CHUNKS + 4):
        piece = own[t * width:(t + 1) * width] if (Z_GATED and t < CHUNKS) else None
        if t > 0:
            gate = {"arrived": arrived[t - 1] if t - 1 < CHUNKS else None}
            if piece is not None:
                gate["piece"] = piece
            if 0 <= t - 2 < CHUNKS:
                gate["block"] = blocks[t - 2]
            if 0 <= t - 3 < CHUNKS:
                gate["summed"] = summed[t - 3]
            if 0 <= t - 4 < CHUNKS:
                gate["gathered"] = gathered[t - 4]
            if total is not None:
                gate["total"] = total
            gate = lax.optimization_barrier(gate)
            if piece is not None:
                piece = gate["piece"]
            if t - 1 < CHUNKS:
                arrived[t - 1] = gate["arrived"]
            if 0 <= t - 2 < CHUNKS:
                blocks[t - 2] = gate["block"]
            if 0 <= t - 3 < CHUNKS:
                summed[t - 3] = gate["summed"]
            if 0 <= t - 4 < CHUNKS:
                gathered[t - 4] = gate["gathered"]
            if total is not None:
                total = gate["total"]
        if piece is not None:
            arrived[t] = shifted_2(piece, "occ", 2)
        c = t - 1
        if 0 <= c < CHUNKS:
            blocks[c], levels[c] = forward(c, arrived[c])
        c = t - 2
        if 0 <= c < CHUNKS:
            summed[c], firsts[c] = reduce(blocks[c])
        c = t - 3
        if 0 <= c < CHUNKS:
            gathered[c] = amplitudes_of(summed[c], firsts[c], levels[c])
        c = t - 4
        if 0 <= c < CHUNKS:
            term = jnp.dot(gathered[c], blocks[c], preferred_element_type=jnp.float32)
            total = term if total is None else total + term
    gamma_own = total
    gamma_back = total
    return (gamma_own + gamma_back).astype(jnp.bfloat16)[None]


def on_device(integrals, occ_energy, vir_energy):
    cycle_size = lax.axis_size("occ")
    if integrals.shape[0] == 1 and 4 % cycle_size == 0 and integrals.shape[1] % (CHUNKS * 8) == 0:
        return paired_plan(integrals, occ_energy, vir_energy)
    return general_plan(integrals, occ_energy, vir_energy)


def solution(mesh):
    placed = (P("occ", "vir", "aux"), P(), P())
    return jax.shard_map(
        on_device, mesh=mesh, in_specs=placed, out_specs=P("occ", "vir", "aux"), check_vma=False
    )
```

```python
import jax
import jax.numpy as jnp
from jax import lax
from jax.sharding import PartitionSpec as P

CHUNKS = 4
AUX_BY_PERMUTE = False
Z_GATED = False


def shifted_2(value, axis, by):
    count = lax.axis_size(axis)
    return lax.ppermute(value, axis, [(i, (i + by) % count) for i in range(count)])


def general_plan(integrals, occ_energy, vir_energy):
    row_count = integrals.shape[0]
    vir_width = integrals.shape[1]
    cycle_size = lax.axis_size("occ")
    position = lax.axis_index("occ")
    own_level = lax.dynamic_slice_in_dim(occ_energy, position * row_count, row_count)
    partner_level = lax.dynamic_slice_in_dim(
        occ_energy, (position - 2) % cycle_size * row_count, row_count
    )
    local_vir = lax.dynamic_slice_in_dim(vir_energy, lax.axis_index("vir") * vir_width, vir_width)
    shifted = shifted_2(integrals, "occ", 2)
    partner = lax.all_gather(shifted, "vir", axis=1, tiled=True)
    virtuals = partner.shape[1]
    pair_level = own_level + partner_level
    share_rows = virtuals // lax.axis_size("aux")
    partial_value = lax.psum_scatter(
        jnp.einsum("nbq,naq->bna", partner, integrals, preferred_element_type=jnp.float32),
        "aux",
        scatter_dimension=0,
        tiled=True,
    )
    first_row = lax.axis_index("aux") * share_rows
    vir_rows = lax.dynamic_slice_in_dim(vir_energy, first_row, share_rows)
    amplitudes = (
        partial_value
        / (pair_level[None, :, None] - vir_rows[:, None, None] - local_vir[None, None, :])
    ).astype(jnp.bfloat16)
    portion = lax.all_gather(amplitudes, "aux", axis=0, tiled=True)
    own_part = jnp.einsum("bna,nbq->naq", portion, partner, preferred_element_type=jnp.float32)
    rows_back = jnp.einsum("bna,naq->nbq", portion, integrals, preferred_element_type=jnp.float32)
    owned = lax.psum_scatter(rows_back, "vir", scatter_dimension=1, tiled=True)
    returned = shifted_2(owned, "occ", -2)
    return (own_part + returned).astype(jnp.bfloat16)


def xor_pairs(count, step):
    return [(j, j ^ step) for j in range(count)]


def aux_reduce_scatter(x):
    count = lax.axis_size("aux")
    k = lax.axis_index("aux")
    first = 0
    step = 1
    while step < count:
        half = x.shape[0] // 2
        bit = (k // step) % 2
        keep = lax.dynamic_slice_in_dim(x, bit * half, half, 0)
        send = lax.dynamic_slice_in_dim(x, (1 - bit) * half, half, 0)
        x = keep + lax.ppermute(send, "aux", xor_pairs(count, step))
        first = first + bit * half
        step *= 2
    return x, first


def aux_all_gather(x):
    count = lax.axis_size("aux")
    k = lax.axis_index("aux")
    step = count // 2
    while step >= 1:
        bit = (k // step) % 2
        other = lax.ppermute(x, "aux", xor_pairs(count, step))
        x = jnp.where(bit == 0, jnp.concatenate([x, other]), jnp.concatenate([other, x]))
        step //= 2
    return x


def paired_plan(integrals, occ_energy, vir_energy):
    own = integrals[0]
    vir_rows, _ = own.shape
    cycle_size = lax.axis_size("occ")
    position = lax.axis_index("occ")
    pair_level = occ_energy[position] + occ_energy[(position - 2) % cycle_size]
    vir_pos = lax.axis_index("vir")
    vir_count = lax.axis_size("vir")
    aux_count = lax.axis_size("aux")
    share = vir_rows // aux_count
    width = vir_rows // CHUNKS
    if not AUX_BY_PERMUTE:
        first_row = lax.axis_index("aux") * share

    def forward(c, arrived):
        if vir_count == 2:
            mate = shifted_2(arrived, "vir", 1)
            block = jnp.concatenate([arrived, mate])
            cols = [vir_pos, 1 - vir_pos]
        else:
            block = lax.all_gather(arrived, "vir", axis=0, tiled=True)
            cols = list(range(vir_count))
        col_level = jnp.concatenate(
            [lax.dynamic_slice_in_dim(vir_energy, w * vir_rows + c * width, width) for w in cols]
        )
        return block, col_level

    def reduce(block):
        partial = jnp.einsum("aq,bq->ab", own, block, preferred_element_type=jnp.float32)
        if AUX_BY_PERMUTE:
            return aux_reduce_scatter(partial)
        return lax.psum_scatter(partial, "aux", scatter_dimension=0, tiled=True), first_row

    def amplitudes_of(summed, first, col_level):
        row_level = lax.dynamic_slice_in_dim(vir_energy, vir_pos * vir_rows + first, share)
        amplitudes = (summed / (pair_level - row_level[:, None] - col_level[None, :])).astype(
            jnp.bfloat16
        )
        if AUX_BY_PERMUTE:
            return aux_all_gather(amplitudes)
        return lax.all_gather(amplitudes, "aux", axis=0, tiled=True)

    arrived = [None] * CHUNKS
    blocks = [None] * CHUNKS
    levels = [None] * CHUNKS
    summed = [None] * CHUNKS
    firsts = [None] * CHUNKS
    gathered = [None] * CHUNKS
    total = None
    for c in range(CHUNKS if not Z_GATED else 0):
        arrived[c] = shifted_2(own[c * width:(c + 1) * width], "occ", 2)
    for t in range(CHUNKS + 4):
        piece = own[t * width:(t + 1) * width] if (Z_GATED and t < CHUNKS) else None
        if t > 0:
            gate = {"arrived": arrived[t - 1] if t - 1 < CHUNKS else None}
            if piece is not None:
                gate["piece"] = piece
            if 0 <= t - 2 < CHUNKS:
                gate["block"] = blocks[t - 2]
            if 0 <= t - 3 < CHUNKS:
                gate["summed"] = summed[t - 3]
            if 0 <= t - 4 < CHUNKS:
                gate["gathered"] = gathered[t - 4]
            if total is not None:
                gate["total"] = total
            gate = lax.optimization_barrier(gate)
            if piece is not None:
                piece = gate["piece"]
            if t - 1 < CHUNKS:
                arrived[t - 1] = gate["arrived"]
            if 0 <= t - 2 < CHUNKS:
                blocks[t - 2] = gate["block"]
            if 0 <= t - 3 < CHUNKS:
                summed[t - 3] = gate["summed"]
            if 0 <= t - 4 < CHUNKS:
                gathered[t - 4] = gate["gathered"]
            if total is not None:
                total = gate["total"]
        if piece is not None:
            arrived[t] = shifted_2(piece, "occ", 2)
        c = t - 1
        if 0 <= c < CHUNKS:
            blocks[c], levels[c] = forward(c, arrived[c])
        c = t - 2
        if 0 <= c < CHUNKS:
            summed[c], firsts[c] = reduce(blocks[c])
        c = t - 3
        if 0 <= c < CHUNKS:
            gathered[c] = amplitudes_of(summed[c], firsts[c], levels[c])
        c = t - 4
        if 0 <= c < CHUNKS:
            term = jnp.dot(gathered[c], blocks[c], preferred_element_type=jnp.float32)
            total = term if total is None else total + term
    gamma_own = total
    gamma_back = total
    return (gamma_own + gamma_back).astype(jnp.bfloat16)[None]


def on_device(integrals, occ_energy, vir_energy):
    cycle_size = lax.axis_size("occ")
    if integrals.shape[0] == 1 and 4 % cycle_size == 0 and integrals.shape[1] % (CHUNKS * 8) == 0:
        return paired_plan(integrals, occ_energy, vir_energy)
    return general_plan(integrals, occ_energy, vir_energy)


def solution(mesh):
    placed = (P("occ", "vir", "aux"), P(), P())
    return jax.shard_map(
        on_device, mesh=mesh, in_specs=placed, out_specs=P("occ", "vir", "aux"), check_vma=False
    )
```

```python
import jax
import jax.numpy as jnp
from jax import lax
from jax.sharding import PartitionSpec as P

CHUNKS = 4
AUX_BY_PERMUTE = True
NARROW_FAR = False


def shifted_2(value, axis, by):
    count = lax.axis_size(axis)
    return lax.ppermute(value, axis, [(i, (i + by) % count) for i in range(count)])


def general_plan(integrals, occ_energy, vir_energy):
    row_count = integrals.shape[0]
    vir_width = integrals.shape[1]
    cycle_size = lax.axis_size("occ")
    position = lax.axis_index("occ")
    own_level = lax.dynamic_slice_in_dim(occ_energy, position * row_count, row_count)
    partner_level = lax.dynamic_slice_in_dim(
        occ_energy, (position - 2) % cycle_size * row_count, row_count
    )
    local_vir = lax.dynamic_slice_in_dim(vir_energy, lax.axis_index("vir") * vir_width, vir_width)
    shifted = shifted_2(integrals, "occ", 2)
    partner = lax.all_gather(shifted, "vir", axis=1, tiled=True)
    virtuals = partner.shape[1]
    pair_level = own_level + partner_level
    share_rows = virtuals // lax.axis_size("aux")
    partial_value = lax.psum_scatter(
        jnp.einsum("nbq,naq->bna", partner, integrals, preferred_element_type=jnp.float32),
        "aux",
        scatter_dimension=0,
        tiled=True,
    )
    first_row = lax.axis_index("aux") * share_rows
    vir_rows = lax.dynamic_slice_in_dim(vir_energy, first_row, share_rows)
    amplitudes = (
        partial_value
        / (pair_level[None, :, None] - vir_rows[:, None, None] - local_vir[None, None, :])
    ).astype(jnp.bfloat16)
    portion = lax.all_gather(amplitudes, "aux", axis=0, tiled=True)
    own_part = jnp.einsum("bna,nbq->naq", portion, partner, preferred_element_type=jnp.float32)
    rows_back = jnp.einsum("bna,naq->nbq", portion, integrals, preferred_element_type=jnp.float32)
    owned = lax.psum_scatter(rows_back, "vir", scatter_dimension=1, tiled=True)
    returned = shifted_2(owned, "occ", -2)
    return (own_part + returned).astype(jnp.bfloat16)


def xor_pairs(count, step):
    return [(j, j ^ step) for j in range(count)]


def aux_reduce_scatter(x):
    count = lax.axis_size("aux")
    k = lax.axis_index("aux")
    first = 0
    step = 1
    while step < count:
        half = x.shape[0] // 2
        bit = (k // step) % 2
        keep = lax.dynamic_slice_in_dim(x, bit * half, half, 0)
        send = lax.dynamic_slice_in_dim(x, (1 - bit) * half, half, 0)
        if step > 1 and NARROW_FAR:
            x = keep + lax.ppermute(send.astype(jnp.bfloat16), "aux", xor_pairs(count, step))
        else:
            x = keep + lax.ppermute(send, "aux", xor_pairs(count, step))
        first = first + bit * half
        step *= 2
    return x, first


def aux_all_gather(x):
    count = lax.axis_size("aux")
    k = lax.axis_index("aux")
    step = count // 2
    while step >= 1:
        bit = (k // step) % 2
        other = lax.ppermute(x, "aux", xor_pairs(count, step))
        x = jnp.where(bit == 0, jnp.concatenate([x, other]), jnp.concatenate([other, x]))
        step //= 2
    return x


def paired_plan(integrals, occ_energy, vir_energy):
    own = integrals[0]
    vir_rows, _ = own.shape
    cycle_size = lax.axis_size("occ")
    position = lax.axis_index("occ")
    pair_level = occ_energy[position] + occ_energy[(position - 2) % cycle_size]
    vir_pos = lax.axis_index("vir")
    vir_count = lax.axis_size("vir")
    aux_count = lax.axis_size("aux")
    share = vir_rows // aux_count
    width = vir_rows // CHUNKS

    if not AUX_BY_PERMUTE:
        first_row = lax.axis_index("aux") * share

    total = None
    previous = None
    rows_done = None
    for c in range(CHUNKS):
        piece = own[c * width:(c + 1) * width]
        if previous is not None:
            piece, _ = lax.optimization_barrier((piece, previous))
        arrived = shifted_2(piece, "occ", 2)
        previous = arrived
        if vir_count == 2:
            mate = shifted_2(arrived, "vir", 1)
            block = jnp.concatenate([arrived, mate])
            cols = [vir_pos, 1 - vir_pos]
        else:
            block = lax.all_gather(arrived, "vir", axis=0, tiled=True)
            cols = list(range(vir_count))
        col_level = jnp.concatenate(
            [lax.dynamic_slice_in_dim(vir_energy, w * vir_rows + c * width, width) for w in cols]
        )
        partial = jnp.einsum("aq,bq->ab", own, block, preferred_element_type=jnp.float32)
        if AUX_BY_PERMUTE:
            summed, first = aux_reduce_scatter(partial)
        else:
            summed = lax.psum_scatter(partial, "aux", scatter_dimension=0, tiled=True)
            first = first_row
        if rows_done is not None:
            summed, _ = lax.optimization_barrier((summed, rows_done))
        row_level = lax.dynamic_slice_in_dim(vir_energy, vir_pos * vir_rows + first, share)
        amplitudes = (summed / (pair_level - row_level[:, None] - col_level[None, :])).astype(
            jnp.bfloat16
        )
        if AUX_BY_PERMUTE:
            rows = aux_all_gather(amplitudes)
        else:
            rows = lax.all_gather(amplitudes, "aux", axis=0, tiled=True)
        rows_done = rows
        term = jnp.dot(rows, block, preferred_element_type=jnp.float32)
        total = term if total is None else total + term
    gamma_own = total
    gamma_back = total
    return (gamma_own + gamma_back).astype(jnp.bfloat16)[None]


def on_device(integrals, occ_energy, vir_energy):
    cycle_size = lax.axis_size("occ")
    if integrals.shape[0] == 1 and 4 % cycle_size == 0 and integrals.shape[1] % (CHUNKS * 8) == 0:
        return paired_plan(integrals, occ_energy, vir_energy)
    return general_plan(integrals, occ_energy, vir_energy)


def solution(mesh):
    placed = (P("occ", "vir", "aux"), P(), P())
    return jax.shard_map(
        on_device, mesh=mesh, in_specs=placed, out_specs=P("occ", "vir", "aux"), check_vma=False
    )
```

```python
import jax
import jax.numpy as jnp
from jax import lax
from jax.sharding import PartitionSpec as P

CHUNKS = 8
AUX_BY_PERMUTE = True
NARROW_FAR = False


def shifted_2(value, axis, by):
    count = lax.axis_size(axis)
    return lax.ppermute(value, axis, [(i, (i + by) % count) for i in range(count)])


def general_plan(integrals, occ_energy, vir_energy):
    row_count = integrals.shape[0]
    vir_width = integrals.shape[1]
    cycle_size = lax.axis_size("occ")
    position = lax.axis_index("occ")
    own_level = lax.dynamic_slice_in_dim(occ_energy, position * row_count, row_count)
    partner_level = lax.dynamic_slice_in_dim(
        occ_energy, (position - 2) % cycle_size * row_count, row_count
    )
    local_vir = lax.dynamic_slice_in_dim(vir_energy, lax.axis_index("vir") * vir_width, vir_width)
    shifted = shifted_2(integrals, "occ", 2)
    partner = lax.all_gather(shifted, "vir", axis=1, tiled=True)
    virtuals = partner.shape[1]
    pair_level = own_level + partner_level
    share_rows = virtuals // lax.axis_size("aux")
    partial_value = lax.psum_scatter(
        jnp.einsum("nbq,naq->bna", partner, integrals, preferred_element_type=jnp.float32),
        "aux",
        scatter_dimension=0,
        tiled=True,
    )
    first_row = lax.axis_index("aux") * share_rows
    vir_rows = lax.dynamic_slice_in_dim(vir_energy, first_row, share_rows)
    amplitudes = (
        partial_value
        / (pair_level[None, :, None] - vir_rows[:, None, None] - local_vir[None, None, :])
    ).astype(jnp.bfloat16)
    portion = lax.all_gather(amplitudes, "aux", axis=0, tiled=True)
    own_part = jnp.einsum("bna,nbq->naq", portion, partner, preferred_element_type=jnp.float32)
    rows_back = jnp.einsum("bna,naq->nbq", portion, integrals, preferred_element_type=jnp.float32)
    owned = lax.psum_scatter(rows_back, "vir", scatter_dimension=1, tiled=True)
    returned = shifted_2(owned, "occ", -2)
    return (own_part + returned).astype(jnp.bfloat16)


def xor_pairs(count, step):
    return [(j, j ^ step) for j in range(count)]


def aux_reduce_scatter(x):
    count = lax.axis_size("aux")
    k = lax.axis_index("aux")
    first = 0
    step = 1
    while step < count:
        half = x.shape[0] // 2
        bit = (k // step) % 2
        keep = lax.dynamic_slice_in_dim(x, bit * half, half, 0)
        send = lax.dynamic_slice_in_dim(x, (1 - bit) * half, half, 0)
        if step > 1 and NARROW_FAR:
            x = keep + lax.ppermute(send.astype(jnp.bfloat16), "aux", xor_pairs(count, step))
        else:
            x = keep + lax.ppermute(send, "aux", xor_pairs(count, step))
        first = first + bit * half
        step *= 2
    return x, first


def aux_all_gather(x):
    count = lax.axis_size("aux")
    k = lax.axis_index("aux")
    step = count // 2
    while step >= 1:
        bit = (k // step) % 2
        other = lax.ppermute(x, "aux", xor_pairs(count, step))
        x = jnp.where(bit == 0, jnp.concatenate([x, other]), jnp.concatenate([other, x]))
        step //= 2
    return x


def paired_plan(integrals, occ_energy, vir_energy):
    own = integrals[0]
    vir_rows, _ = own.shape
    cycle_size = lax.axis_size("occ")
    position = lax.axis_index("occ")
    pair_level = occ_energy[position] + occ_energy[(position - 2) % cycle_size]
    vir_pos = lax.axis_index("vir")
    vir_count = lax.axis_size("vir")
    aux_count = lax.axis_size("aux")
    share = vir_rows // aux_count
    width = vir_rows // CHUNKS

    if not AUX_BY_PERMUTE:
        first_row = lax.axis_index("aux") * share

    total = None
    previous = None
    rows_done = None
    for c in range(CHUNKS):
        piece = own[c * width:(c + 1) * width]
        if previous is not None:
            piece, _ = lax.optimization_barrier((piece, previous))
        arrived = shifted_2(piece, "occ", 2)
        previous = arrived
        if vir_count == 2:
            mate = shifted_2(arrived, "vir", 1)
            block = jnp.concatenate([arrived, mate])
            cols = [vir_pos, 1 - vir_pos]
        else:
            block = lax.all_gather(arrived, "vir", axis=0, tiled=True)
            cols = list(range(vir_count))
        col_level = jnp.concatenate(
            [lax.dynamic_slice_in_dim(vir_energy, w * vir_rows + c * width, width) for w in cols]
        )
        partial = jnp.einsum("aq,bq->ab", own, block, preferred_element_type=jnp.float32)
        if AUX_BY_PERMUTE:
            summed, first = aux_reduce_scatter(partial)
        else:
            summed = lax.psum_scatter(partial, "aux", scatter_dimension=0, tiled=True)
            first = first_row
        if rows_done is not None:
            summed, _ = lax.optimization_barrier((summed, rows_done))
        row_level = lax.dynamic_slice_in_dim(vir_energy, vir_pos * vir_rows + first, share)
        amplitudes = (summed / (pair_level - row_level[:, None] - col_level[None, :])).astype(
            jnp.bfloat16
        )
        if AUX_BY_PERMUTE:
            rows = aux_all_gather(amplitudes)
        else:
            rows = lax.all_gather(amplitudes, "aux", axis=0, tiled=True)
        rows_done = rows
        term = jnp.dot(rows, block, preferred_element_type=jnp.float32)
        total = term if total is None else total + term
    gamma_own = total
    gamma_back = total
    return (gamma_own + gamma_back).astype(jnp.bfloat16)[None]


def on_device(integrals, occ_energy, vir_energy):
    cycle_size = lax.axis_size("occ")
    if integrals.shape[0] == 1 and 4 % cycle_size == 0 and integrals.shape[1] % (CHUNKS * 8) == 0:
        return paired_plan(integrals, occ_energy, vir_energy)
    return general_plan(integrals, occ_energy, vir_energy)


def solution(mesh):
    placed = (P("occ", "vir", "aux"), P(), P())
    return jax.shard_map(
        on_device, mesh=mesh, in_specs=placed, out_specs=P("occ", "vir", "aux"), check_vma=False
    )
```

```python
import jax
import jax.numpy as jnp
from jax import lax
from jax.sharding import PartitionSpec as P

CHUNKS = 4
AUX_BY_PERMUTE = True
NARROW_FAR = False


def shifted_2(value, axis, by):
    count = lax.axis_size(axis)
    return lax.ppermute(value, axis, [(i, (i + by) % count) for i in range(count)])


def general_plan(integrals, occ_energy, vir_energy):
    row_count = integrals.shape[0]
    vir_width = integrals.shape[1]
    cycle_size = lax.axis_size("occ")
    position = lax.axis_index("occ")
    own_level = lax.dynamic_slice_in_dim(occ_energy, position * row_count, row_count)
    partner_level = lax.dynamic_slice_in_dim(
        occ_energy, (position - 2) % cycle_size * row_count, row_count
    )
    local_vir = lax.dynamic_slice_in_dim(vir_energy, lax.axis_index("vir") * vir_width, vir_width)
    shifted = shifted_2(integrals, "occ", 2)
    partner = lax.all_gather(shifted, "vir", axis=1, tiled=True)
    virtuals = partner.shape[1]
    pair_level = own_level + partner_level
    share_rows = virtuals // lax.axis_size("aux")
    partial_value = lax.psum_scatter(
        jnp.einsum("nbq,naq->bna", partner, integrals, preferred_element_type=jnp.float32),
        "aux",
        scatter_dimension=0,
        tiled=True,
    )
    first_row = lax.axis_index("aux") * share_rows
    vir_rows = lax.dynamic_slice_in_dim(vir_energy, first_row, share_rows)
    amplitudes = (
        partial_value
        / (pair_level[None, :, None] - vir_rows[:, None, None] - local_vir[None, None, :])
    ).astype(jnp.bfloat16)
    portion = lax.all_gather(amplitudes, "aux", axis=0, tiled=True)
    own_part = jnp.einsum("bna,nbq->naq", portion, partner, preferred_element_type=jnp.float32)
    rows_back = jnp.einsum("bna,naq->nbq", portion, integrals, preferred_element_type=jnp.float32)
    owned = lax.psum_scatter(rows_back, "vir", scatter_dimension=1, tiled=True)
    returned = shifted_2(owned, "occ", -2)
    return (own_part + returned).astype(jnp.bfloat16)


def xor_pairs(count, step):
    return [(j, j ^ step) for j in range(count)]


def aux_reduce_scatter(x, first=0, step=1, stop=None):
    count = lax.axis_size("aux")
    k = lax.axis_index("aux")
    stop = count if stop is None else stop
    while step < stop:
        half = x.shape[0] // 2
        bit = (k // step) % 2
        keep = lax.dynamic_slice_in_dim(x, bit * half, half, 0)
        send = lax.dynamic_slice_in_dim(x, (1 - bit) * half, half, 0)
        if step > 1 and NARROW_FAR:
            x = keep + lax.ppermute(send.astype(jnp.bfloat16), "aux", xor_pairs(count, step))
        else:
            x = keep + lax.ppermute(send, "aux", xor_pairs(count, step))
        first = first + bit * half
        step *= 2
    return x, first


def aux_all_gather(x):
    count = lax.axis_size("aux")
    k = lax.axis_index("aux")
    step = count // 2
    while step >= 1:
        bit = (k // step) % 2
        other = lax.ppermute(x, "aux", xor_pairs(count, step))
        x = jnp.where(bit == 0, jnp.concatenate([x, other]), jnp.concatenate([other, x]))
        step //= 2
    return x


def paired_plan(integrals, occ_energy, vir_energy):
    own = integrals[0]
    vir_rows, _ = own.shape
    cycle_size = lax.axis_size("occ")
    position = lax.axis_index("occ")
    pair_level = occ_energy[position] + occ_energy[(position - 2) % cycle_size]
    vir_pos = lax.axis_index("vir")
    vir_count = lax.axis_size("vir")
    aux_count = lax.axis_size("aux")
    share = vir_rows // aux_count
    width = vir_rows // CHUNKS

    if not AUX_BY_PERMUTE:
        first_row = lax.axis_index("aux") * share

    total = None
    previous = None
    rows_done = None
    near, far = [], []
    for c in range(CHUNKS):
        piece = own[c * width:(c + 1) * width]
        if previous is not None:
            gate = [previous] + [s for s in (near[c - 2:c - 1] + far[c - 3:c - 2]) if c >= 2]
            piece, _ = lax.optimization_barrier((piece, gate))
        arrived = shifted_2(piece, "occ", 2)
        previous = arrived
        if vir_count == 2:
            mate = shifted_2(arrived, "vir", 1)
            block = jnp.concatenate([arrived, mate])
            cols = [vir_pos, 1 - vir_pos]
        else:
            block = lax.all_gather(arrived, "vir", axis=0, tiled=True)
            cols = list(range(vir_count))
        col_level = jnp.concatenate(
            [lax.dynamic_slice_in_dim(vir_energy, w * vir_rows + c * width, width) for w in cols]
        )
        partial = jnp.einsum("aq,bq->ab", own, block, preferred_element_type=jnp.float32)
        if AUX_BY_PERMUTE:
            summed, first = aux_reduce_scatter(partial, stop=2)
            near.append(summed)
            summed, first = aux_reduce_scatter(summed, first, step=2)
            far.append(summed)
        else:
            summed = lax.psum_scatter(partial, "aux", scatter_dimension=0, tiled=True)
            first = first_row
        if rows_done is not None:
            summed, _ = lax.optimization_barrier((summed, rows_done))
        row_level = lax.dynamic_slice_in_dim(vir_energy, vir_pos * vir_rows + first, share)
        amplitudes = (summed / (pair_level - row_level[:, None] - col_level[None, :])).astype(
            jnp.bfloat16
        )
        if AUX_BY_PERMUTE:
            rows = aux_all_gather(amplitudes)
        else:
            rows = lax.all_gather(amplitudes, "aux", axis=0, tiled=True)
        rows_done = rows
        term = jnp.dot(rows, block, preferred_element_type=jnp.float32)
        total = term if total is None else total + term
    gamma_own = total
    gamma_back = total
    return (gamma_own + gamma_back).astype(jnp.bfloat16)[None]


def on_device(integrals, occ_energy, vir_energy):
    cycle_size = lax.axis_size("occ")
    if integrals.shape[0] == 1 and 4 % cycle_size == 0 and integrals.shape[1] % (CHUNKS * 8) == 0:
        return paired_plan(integrals, occ_energy, vir_energy)
    return general_plan(integrals, occ_energy, vir_energy)


def solution(mesh):
    placed = (P("occ", "vir", "aux"), P(), P())
    return jax.shard_map(
        on_device, mesh=mesh, in_specs=placed, out_specs=P("occ", "vir", "aux"), check_vma=False
    )
```

```python
import jax
import jax.numpy as jnp
from jax import lax
from jax.sharding import PartitionSpec as P

CHUNKS = 4
AUX_BY_PERMUTE = True
NARROW_FAR = False


def shifted_2(value, axis, by):
    count = lax.axis_size(axis)
    return lax.ppermute(value, axis, [(i, (i + by) % count) for i in range(count)])


def general_plan(integrals, occ_energy, vir_energy):
    row_count = integrals.shape[0]
    vir_width = integrals.shape[1]
    cycle_size = lax.axis_size("occ")
    position = lax.axis_index("occ")
    own_level = lax.dynamic_slice_in_dim(occ_energy, position * row_count, row_count)
    partner_level = lax.dynamic_slice_in_dim(
        occ_energy, (position - 2) % cycle_size * row_count, row_count
    )
    local_vir = lax.dynamic_slice_in_dim(vir_energy, lax.axis_index("vir") * vir_width, vir_width)
    shifted = shifted_2(integrals, "occ", 2)
    partner = lax.all_gather(shifted, "vir", axis=1, tiled=True)
    virtuals = partner.shape[1]
    pair_level = own_level + partner_level
    share_rows = virtuals // lax.axis_size("aux")
    partial_value = lax.psum_scatter(
        jnp.einsum("nbq,naq->bna", partner, integrals, preferred_element_type=jnp.float32),
        "aux",
        scatter_dimension=0,
        tiled=True,
    )
    first_row = lax.axis_index("aux") * share_rows
    vir_rows = lax.dynamic_slice_in_dim(vir_energy, first_row, share_rows)
    amplitudes = (
        partial_value
        / (pair_level[None, :, None] - vir_rows[:, None, None] - local_vir[None, None, :])
    ).astype(jnp.bfloat16)
    portion = lax.all_gather(amplitudes, "aux", axis=0, tiled=True)
    own_part = jnp.einsum("bna,nbq->naq", portion, partner, preferred_element_type=jnp.float32)
    rows_back = jnp.einsum("bna,naq->nbq", portion, integrals, preferred_element_type=jnp.float32)
    owned = lax.psum_scatter(rows_back, "vir", scatter_dimension=1, tiled=True)
    returned = shifted_2(owned, "occ", -2)
    return (own_part + returned).astype(jnp.bfloat16)


def xor_pairs(count, step):
    return [(j, j ^ step) for j in range(count)]


def aux_reduce_scatter(x):
    count = lax.axis_size("aux")
    k = lax.axis_index("aux")
    first = 0
    step = 1
    while step < count:
        half = x.shape[0] // 2
        bit = (k // step) % 2
        keep = lax.dynamic_slice_in_dim(x, bit * half, half, 0)
        send = lax.dynamic_slice_in_dim(x, (1 - bit) * half, half, 0)
        if step > 1 and NARROW_FAR:
            x = keep + lax.ppermute(send.astype(jnp.bfloat16), "aux", xor_pairs(count, step))
        else:
            x = keep + lax.ppermute(send, "aux", xor_pairs(count, step))
        first = first + bit * half
        step *= 2
    return x, first


def aux_all_gather(x):
    count = lax.axis_size("aux")
    k = lax.axis_index("aux")
    step = count // 2
    while step >= 1:
        bit = (k // step) % 2
        other = lax.ppermute(x, "aux", xor_pairs(count, step))
        x = jnp.where(bit == 0, jnp.concatenate([x, other]), jnp.concatenate([other, x]))
        step //= 2
    return x


def paired_plan(integrals, occ_energy, vir_energy):
    own = integrals[0]
    vir_rows, _ = own.shape
    cycle_size = lax.axis_size("occ")
    position = lax.axis_index("occ")
    pair_level = occ_energy[position] + occ_energy[(position - 2) % cycle_size]
    vir_pos = lax.axis_index("vir")
    vir_count = lax.axis_size("vir")
    aux_count = lax.axis_size("aux")
    share = vir_rows // aux_count
    width = vir_rows // CHUNKS

    if not AUX_BY_PERMUTE:
        first_row = lax.axis_index("aux") * share

    total = None
    previous = None
    rows_done = None
    for c in range(CHUNKS):
        piece = own[c * width:(c + 1) * width]
        if previous is not None:
            piece, _ = lax.optimization_barrier((piece, previous))
        arrived = shifted_2(piece, "occ", 2)
        previous = arrived
        if vir_count == 2:
            mate = shifted_2(arrived, "vir", 1)
            block = jnp.concatenate([arrived, mate])
            cols = [vir_pos, 1 - vir_pos]
        else:
            block = lax.all_gather(arrived, "vir", axis=0, tiled=True)
            cols = list(range(vir_count))
        col_level = jnp.concatenate(
            [lax.dynamic_slice_in_dim(vir_energy, w * vir_rows + c * width, width) for w in cols]
        )
        partial = jnp.einsum("aq,bq->ab", own, block, preferred_element_type=jnp.float32)
        if AUX_BY_PERMUTE:
            summed, first = aux_reduce_scatter(partial)
        else:
            summed = lax.psum_scatter(partial, "aux", scatter_dimension=0, tiled=True)
            first = first_row
        if rows_done is not None:
            summed, _ = lax.optimization_barrier((summed, (rows_done, total)))
        row_level = lax.dynamic_slice_in_dim(vir_energy, vir_pos * vir_rows + first, share)
        amplitudes = (summed / (pair_level - row_level[:, None] - col_level[None, :])).astype(
            jnp.bfloat16
        )
        if AUX_BY_PERMUTE:
            rows = aux_all_gather(amplitudes)
        else:
            rows = lax.all_gather(amplitudes, "aux", axis=0, tiled=True)
        rows_done = rows
        term = jnp.dot(rows, block, preferred_element_type=jnp.float32)
        total = term if total is None else total + term
    gamma_own = total
    gamma_back = total
    return (gamma_own + gamma_back).astype(jnp.bfloat16)[None]


def on_device(integrals, occ_energy, vir_energy):
    cycle_size = lax.axis_size("occ")
    if integrals.shape[0] == 1 and 4 % cycle_size == 0 and integrals.shape[1] % (CHUNKS * 8) == 0:
        return paired_plan(integrals, occ_energy, vir_energy)
    return general_plan(integrals, occ_energy, vir_energy)


def solution(mesh):
    placed = (P("occ", "vir", "aux"), P(), P())
    return jax.shard_map(
        on_device, mesh=mesh, in_specs=placed, out_specs=P("occ", "vir", "aux"), check_vma=False
    )
```

```python
import jax
import jax.numpy as jnp
from jax import lax
from jax.sharding import PartitionSpec as P

CHUNKS = 4
AUX_BY_PERMUTE = True
NARROW_FAR = False
Z_DEPTH = 2


def shifted_2(value, axis, by):
    count = lax.axis_size(axis)
    return lax.ppermute(value, axis, [(i, (i + by) % count) for i in range(count)])


def general_plan(integrals, occ_energy, vir_energy):
    row_count = integrals.shape[0]
    vir_width = integrals.shape[1]
    cycle_size = lax.axis_size("occ")
    position = lax.axis_index("occ")
    own_level = lax.dynamic_slice_in_dim(occ_energy, position * row_count, row_count)
    partner_level = lax.dynamic_slice_in_dim(
        occ_energy, (position - 2) % cycle_size * row_count, row_count
    )
    local_vir = lax.dynamic_slice_in_dim(vir_energy, lax.axis_index("vir") * vir_width, vir_width)
    shifted = shifted_2(integrals, "occ", 2)
    partner = lax.all_gather(shifted, "vir", axis=1, tiled=True)
    virtuals = partner.shape[1]
    pair_level = own_level + partner_level
    share_rows = virtuals // lax.axis_size("aux")
    partial_value = lax.psum_scatter(
        jnp.einsum("nbq,naq->bna", partner, integrals, preferred_element_type=jnp.float32),
        "aux",
        scatter_dimension=0,
        tiled=True,
    )
    first_row = lax.axis_index("aux") * share_rows
    vir_rows = lax.dynamic_slice_in_dim(vir_energy, first_row, share_rows)
    amplitudes = (
        partial_value
        / (pair_level[None, :, None] - vir_rows[:, None, None] - local_vir[None, None, :])
    ).astype(jnp.bfloat16)
    portion = lax.all_gather(amplitudes, "aux", axis=0, tiled=True)
    own_part = jnp.einsum("bna,nbq->naq", portion, partner, preferred_element_type=jnp.float32)
    rows_back = jnp.einsum("bna,naq->nbq", portion, integrals, preferred_element_type=jnp.float32)
    owned = lax.psum_scatter(rows_back, "vir", scatter_dimension=1, tiled=True)
    returned = shifted_2(owned, "occ", -2)
    return (own_part + returned).astype(jnp.bfloat16)


def xor_pairs(count, step):
    return [(j, j ^ step) for j in range(count)]


def aux_reduce_scatter(x):
    count = lax.axis_size("aux")
    k = lax.axis_index("aux")
    first = 0
    step = 1
    while step < count:
        half = x.shape[0] // 2
        bit = (k // step) % 2
        keep = lax.dynamic_slice_in_dim(x, bit * half, half, 0)
        send = lax.dynamic_slice_in_dim(x, (1 - bit) * half, half, 0)
        if step > 1 and NARROW_FAR:
            x = keep + lax.ppermute(send.astype(jnp.bfloat16), "aux", xor_pairs(count, step))
        else:
            x = keep + lax.ppermute(send, "aux", xor_pairs(count, step))
        first = first + bit * half
        step *= 2
    return x, first


def aux_all_gather(x):
    count = lax.axis_size("aux")
    k = lax.axis_index("aux")
    step = count // 2
    while step >= 1:
        bit = (k // step) % 2
        other = lax.ppermute(x, "aux", xor_pairs(count, step))
        x = jnp.where(bit == 0, jnp.concatenate([x, other]), jnp.concatenate([other, x]))
        step //= 2
    return x


def paired_plan(integrals, occ_energy, vir_energy):
    own = integrals[0]
    vir_rows, _ = own.shape
    cycle_size = lax.axis_size("occ")
    position = lax.axis_index("occ")
    pair_level = occ_energy[position] + occ_energy[(position - 2) % cycle_size]
    vir_pos = lax.axis_index("vir")
    vir_count = lax.axis_size("vir")
    aux_count = lax.axis_size("aux")
    share = vir_rows // aux_count
    width = vir_rows // CHUNKS

    if not AUX_BY_PERMUTE:
        first_row = lax.axis_index("aux") * share

    total = None
    landed = []
    rows_done = None
    for c in range(CHUNKS):
        piece = own[c * width:(c + 1) * width]
        if c >= Z_DEPTH:
            piece, _ = lax.optimization_barrier((piece, landed[c - Z_DEPTH]))
        arrived = shifted_2(piece, "occ", 2)
        landed.append(arrived)
        if vir_count == 2:
            mate = shifted_2(arrived, "vir", 1)
            block = jnp.concatenate([arrived, mate])
            cols = [vir_pos, 1 - vir_pos]
        else:
            block = lax.all_gather(arrived, "vir", axis=0, tiled=True)
            cols = list(range(vir_count))
        col_level = jnp.concatenate(
            [lax.dynamic_slice_in_dim(vir_energy, w * vir_rows + c * width, width) for w in cols]
        )
        partial = jnp.einsum("aq,bq->ab", own, block, preferred_element_type=jnp.float32)
        if AUX_BY_PERMUTE:
            summed, first = aux_reduce_scatter(partial)
        else:
            summed = lax.psum_scatter(partial, "aux", scatter_dimension=0, tiled=True)
            first = first_row
        if rows_done is not None:
            summed, _ = lax.optimization_barrier((summed, rows_done))
        row_level = lax.dynamic_slice_in_dim(vir_energy, vir_pos * vir_rows + first, share)
        amplitudes = (summed / (pair_level - row_level[:, None] - col_level[None, :])).astype(
            jnp.bfloat16
        )
        if AUX_BY_PERMUTE:
            rows = aux_all_gather(amplitudes)
        else:
            rows = lax.all_gather(amplitudes, "aux", axis=0, tiled=True)
        rows_done = rows
        term = jnp.dot(rows, block, preferred_element_type=jnp.float32)
        total = term if total is None else total + term
    gamma_own = total
    gamma_back = total
    return (gamma_own + gamma_back).astype(jnp.bfloat16)[None]


def on_device(integrals, occ_energy, vir_energy):
    cycle_size = lax.axis_size("occ")
    if integrals.shape[0] == 1 and 4 % cycle_size == 0 and integrals.shape[1] % (CHUNKS * 8) == 0:
        return paired_plan(integrals, occ_energy, vir_energy)
    return general_plan(integrals, occ_energy, vir_energy)


def solution(mesh):
    placed = (P("occ", "vir", "aux"), P(), P())
    return jax.shard_map(
        on_device, mesh=mesh, in_specs=placed, out_specs=P("occ", "vir", "aux"), check_vma=False
    )
```

```python
import jax
import jax.numpy as jnp
from jax import lax
from jax.sharding import Mesh, PartitionSpec as P

CHUNKS = 4
AUX_BY_PERMUTE = True
NARROW_FAR = False
Z_BY_GATHER = True


def shifted_2(value, axis, by):
    count = lax.axis_size(axis)
    return lax.ppermute(value, axis, [(i, (i + by) % count) for i in range(count)])


def general_plan(integrals, occ_energy, vir_energy):
    row_count = integrals.shape[0]
    vir_width = integrals.shape[1]
    cycle_size = lax.axis_size("occ")
    position = lax.axis_index("occ")
    own_level = lax.dynamic_slice_in_dim(occ_energy, position * row_count, row_count)
    partner_level = lax.dynamic_slice_in_dim(
        occ_energy, (position - 2) % cycle_size * row_count, row_count
    )
    local_vir = lax.dynamic_slice_in_dim(vir_energy, lax.axis_index("vir") * vir_width, vir_width)
    shifted = shifted_2(integrals, "occ", 2)
    partner = lax.all_gather(shifted, "vir", axis=1, tiled=True)
    virtuals = partner.shape[1]
    pair_level = own_level + partner_level
    share_rows = virtuals // lax.axis_size("aux")
    partial_value = lax.psum_scatter(
        jnp.einsum("nbq,naq->bna", partner, integrals, preferred_element_type=jnp.float32),
        "aux",
        scatter_dimension=0,
        tiled=True,
    )
    first_row = lax.axis_index("aux") * share_rows
    vir_rows = lax.dynamic_slice_in_dim(vir_energy, first_row, share_rows)
    amplitudes = (
        partial_value
        / (pair_level[None, :, None] - vir_rows[:, None, None] - local_vir[None, None, :])
    ).astype(jnp.bfloat16)
    portion = lax.all_gather(amplitudes, "aux", axis=0, tiled=True)
    own_part = jnp.einsum("bna,nbq->naq", portion, partner, preferred_element_type=jnp.float32)
    rows_back = jnp.einsum("bna,naq->nbq", portion, integrals, preferred_element_type=jnp.float32)
    owned = lax.psum_scatter(rows_back, "vir", scatter_dimension=1, tiled=True)
    returned = shifted_2(owned, "occ", -2)
    return (own_part + returned).astype(jnp.bfloat16)


def xor_pairs(count, step):
    return [(j, j ^ step) for j in range(count)]


def aux_reduce_scatter(x):
    count = lax.axis_size("aux")
    k = lax.axis_index("aux")
    first = 0
    step = 1
    while step < count:
        half = x.shape[0] // 2
        bit = (k // step) % 2
        keep = lax.dynamic_slice_in_dim(x, bit * half, half, 0)
        send = lax.dynamic_slice_in_dim(x, (1 - bit) * half, half, 0)
        if step > 1 and NARROW_FAR:
            x = keep + lax.ppermute(send.astype(jnp.bfloat16), "aux", xor_pairs(count, step))
        else:
            x = keep + lax.ppermute(send, "aux", xor_pairs(count, step))
        first = first + bit * half
        step *= 2
    return x, first


def aux_all_gather(x):
    count = lax.axis_size("aux")
    k = lax.axis_index("aux")
    step = count // 2
    while step >= 1:
        bit = (k // step) % 2
        other = lax.ppermute(x, "aux", xor_pairs(count, step))
        x = jnp.where(bit == 0, jnp.concatenate([x, other]), jnp.concatenate([other, x]))
        step //= 2
    return x


def paired_plan(integrals, occ_energy, vir_energy, occ="occ", gather_z=False):
    own = integrals[0]
    vir_rows, _ = own.shape
    cycle_size = lax.axis_size(occ)
    position = lax.axis_index(occ)
    pair_level = occ_energy[position] + occ_energy[(position - 2) % cycle_size]
    vir_pos = lax.axis_index("vir")
    vir_count = lax.axis_size("vir")
    aux_count = lax.axis_size("aux")
    share = vir_rows // aux_count
    width = vir_rows // CHUNKS

    if not AUX_BY_PERMUTE:
        first_row = lax.axis_index("aux") * share

    total = None
    previous = None
    rows_done = None
    for c in range(CHUNKS):
        piece = own[c * width:(c + 1) * width]
        if gather_z:
            pair = lax.all_gather(piece, "occ_hi", axis=0)
            arrived = lax.dynamic_index_in_dim(pair, 1 - lax.axis_index("occ_hi"), 0, False)
        else:
            if previous is not None:
                piece, _ = lax.optimization_barrier((piece, previous))
            arrived = shifted_2(piece, "occ", 2)
            previous = arrived
        if vir_count == 2:
            mate = shifted_2(arrived, "vir", 1)
            block = jnp.concatenate([arrived, mate])
            cols = [vir_pos, 1 - vir_pos]
        else:
            block = lax.all_gather(arrived, "vir", axis=0, tiled=True)
            cols = list(range(vir_count))
        col_level = jnp.concatenate(
            [lax.dynamic_slice_in_dim(vir_energy, w * vir_rows + c * width, width) for w in cols]
        )
        partial = jnp.einsum("aq,bq->ab", own, block, preferred_element_type=jnp.float32)
        if AUX_BY_PERMUTE:
            summed, first = aux_reduce_scatter(partial)
        else:
            summed = lax.psum_scatter(partial, "aux", scatter_dimension=0, tiled=True)
            first = first_row
        if rows_done is not None:
            summed, _ = lax.optimization_barrier((summed, rows_done))
        row_level = lax.dynamic_slice_in_dim(vir_energy, vir_pos * vir_rows + first, share)
        amplitudes = (summed / (pair_level - row_level[:, None] - col_level[None, :])).astype(
            jnp.bfloat16
        )
        if AUX_BY_PERMUTE:
            rows = aux_all_gather(amplitudes)
        else:
            rows = lax.all_gather(amplitudes, "aux", axis=0, tiled=True)
        rows_done = rows
        term = jnp.dot(rows, block, preferred_element_type=jnp.float32)
        total = term if total is None else total + term
    gamma_own = total
    gamma_back = total
    return (gamma_own + gamma_back).astype(jnp.bfloat16)[None]


def on_device(integrals, occ_energy, vir_energy):
    cycle_size = lax.axis_size("occ")
    if integrals.shape[0] == 1 and 4 % cycle_size == 0 and integrals.shape[1] % (CHUNKS * 8) == 0:
        return paired_plan(integrals, occ_energy, vir_energy)
    return general_plan(integrals, occ_energy, vir_energy)


def solution(mesh):
    if Z_BY_GATHER and mesh.shape["occ"] == 4:
        names = list(mesh.axis_names)
        at = names.index("occ")
        devices = mesh.devices.reshape(
            mesh.devices.shape[:at] + (2, 2) + mesh.devices.shape[at + 1:]
        )
        split = Mesh(devices, tuple(names[:at] + ["occ_hi", "occ_lo"] + names[at + 1:]))
        occ = ("occ_hi", "occ_lo")
        spec = P(occ, "vir", "aux")
        return jax.shard_map(
            paired_on_split, mesh=split, in_specs=(spec, P(), P()), out_specs=spec,
            check_vma=False,
        )
    placed = (P("occ", "vir", "aux"), P(), P())
    return jax.shard_map(
        on_device, mesh=mesh, in_specs=placed, out_specs=P("occ", "vir", "aux"), check_vma=False
    )


def paired_on_split(integrals, occ_energy, vir_energy):
    return paired_plan(integrals, occ_energy, vir_energy, ("occ_hi", "occ_lo"), True)
```

```python
import jax
import jax.numpy as jnp
from jax import lax
from jax.sharding import PartitionSpec as P

WIDTHS = (128, 384, 384, 128)
AUX_BY_PERMUTE = True
NARROW_FAR = False


def shifted_2(value, axis, by):
    count = lax.axis_size(axis)
    return lax.ppermute(value, axis, [(i, (i + by) % count) for i in range(count)])


def general_plan(integrals, occ_energy, vir_energy):
    row_count = integrals.shape[0]
    vir_width = integrals.shape[1]
    cycle_size = lax.axis_size("occ")
    position = lax.axis_index("occ")
    own_level = lax.dynamic_slice_in_dim(occ_energy, position * row_count, row_count)
    partner_level = lax.dynamic_slice_in_dim(
        occ_energy, (position - 2) % cycle_size * row_count, row_count
    )
    local_vir = lax.dynamic_slice_in_dim(vir_energy, lax.axis_index("vir") * vir_width, vir_width)
    shifted = shifted_2(integrals, "occ", 2)
    partner = lax.all_gather(shifted, "vir", axis=1, tiled=True)
    virtuals = partner.shape[1]
    pair_level = own_level + partner_level
    share_rows = virtuals // lax.axis_size("aux")
    partial_value = lax.psum_scatter(
        jnp.einsum("nbq,naq->bna", partner, integrals, preferred_element_type=jnp.float32),
        "aux",
        scatter_dimension=0,
        tiled=True,
    )
    first_row = lax.axis_index("aux") * share_rows
    vir_rows = lax.dynamic_slice_in_dim(vir_energy, first_row, share_rows)
    amplitudes = (
        partial_value
        / (pair_level[None, :, None] - vir_rows[:, None, None] - local_vir[None, None, :])
    ).astype(jnp.bfloat16)
    portion = lax.all_gather(amplitudes, "aux", axis=0, tiled=True)
    own_part = jnp.einsum("bna,nbq->naq", portion, partner, preferred_element_type=jnp.float32)
    rows_back = jnp.einsum("bna,naq->nbq", portion, integrals, preferred_element_type=jnp.float32)
    owned = lax.psum_scatter(rows_back, "vir", scatter_dimension=1, tiled=True)
    returned = shifted_2(owned, "occ", -2)
    return (own_part + returned).astype(jnp.bfloat16)


def xor_pairs(count, step):
    return [(j, j ^ step) for j in range(count)]


def aux_reduce_scatter(x):
    count = lax.axis_size("aux")
    k = lax.axis_index("aux")
    first = 0
    step = 1
    while step < count:
        half = x.shape[0] // 2
        bit = (k // step) % 2
        keep = lax.dynamic_slice_in_dim(x, bit * half, half, 0)
        send = lax.dynamic_slice_in_dim(x, (1 - bit) * half, half, 0)
        if step > 1 and NARROW_FAR:
            x = keep + lax.ppermute(send.astype(jnp.bfloat16), "aux", xor_pairs(count, step))
        else:
            x = keep + lax.ppermute(send, "aux", xor_pairs(count, step))
        first = first + bit * half
        step *= 2
    return x, first


def aux_all_gather(x):
    count = lax.axis_size("aux")
    k = lax.axis_index("aux")
    step = count // 2
    while step >= 1:
        bit = (k // step) % 2
        other = lax.ppermute(x, "aux", xor_pairs(count, step))
        x = jnp.where(bit == 0, jnp.concatenate([x, other]), jnp.concatenate([other, x]))
        step //= 2
    return x


def paired_plan(integrals, occ_energy, vir_energy):
    own = integrals[0]
    vir_rows, _ = own.shape
    cycle_size = lax.axis_size("occ")
    position = lax.axis_index("occ")
    pair_level = occ_energy[position] + occ_energy[(position - 2) % cycle_size]
    vir_pos = lax.axis_index("vir")
    vir_count = lax.axis_size("vir")
    aux_count = lax.axis_size("aux")
    share = vir_rows // aux_count
    widths = [w * (vir_rows // sum(WIDTHS)) for w in WIDTHS]
    starts = [sum(widths[:c]) for c in range(len(widths))]

    if not AUX_BY_PERMUTE:
        first_row = lax.axis_index("aux") * share

    total = None
    previous = None
    rows_done = None
    for c, width in enumerate(widths):
        piece = own[starts[c]:starts[c] + width]
        if previous is not None:
            piece, _ = lax.optimization_barrier((piece, previous))
        arrived = shifted_2(piece, "occ", 2)
        previous = arrived
        if vir_count == 2:
            mate = shifted_2(arrived, "vir", 1)
            block = jnp.concatenate([arrived, mate])
            cols = [vir_pos, 1 - vir_pos]
        else:
            block = lax.all_gather(arrived, "vir", axis=0, tiled=True)
            cols = list(range(vir_count))
        col_level = jnp.concatenate(
            [lax.dynamic_slice_in_dim(vir_energy, w * vir_rows + starts[c], width) for w in cols]
        )
        partial = jnp.einsum("aq,bq->ab", own, block, preferred_element_type=jnp.float32)
        if AUX_BY_PERMUTE:
            summed, first = aux_reduce_scatter(partial)
        else:
            summed = lax.psum_scatter(partial, "aux", scatter_dimension=0, tiled=True)
            first = first_row
        if rows_done is not None:
            summed, _ = lax.optimization_barrier((summed, rows_done))
        row_level = lax.dynamic_slice_in_dim(vir_energy, vir_pos * vir_rows + first, share)
        amplitudes = (summed / (pair_level - row_level[:, None] - col_level[None, :])).astype(
            jnp.bfloat16
        )
        if AUX_BY_PERMUTE:
            rows = aux_all_gather(amplitudes)
        else:
            rows = lax.all_gather(amplitudes, "aux", axis=0, tiled=True)
        rows_done = rows
        term = jnp.dot(rows, block, preferred_element_type=jnp.float32)
        total = term if total is None else total + term
    gamma_own = total
    gamma_back = total
    return (gamma_own + gamma_back).astype(jnp.bfloat16)[None]


def on_device(integrals, occ_energy, vir_energy):
    cycle_size = lax.axis_size("occ")
    if integrals.shape[0] == 1 and 4 % cycle_size == 0 and integrals.shape[1] % sum(WIDTHS) == 0:
        return paired_plan(integrals, occ_energy, vir_energy)
    return general_plan(integrals, occ_energy, vir_energy)


def solution(mesh):
    placed = (P("occ", "vir", "aux"), P(), P())
    return jax.shard_map(
        on_device, mesh=mesh, in_specs=placed, out_specs=P("occ", "vir", "aux"), check_vma=False
    )
```

```python
import jax
import jax.numpy as jnp
from jax import lax
from jax.sharding import PartitionSpec as P

CHUNKS = 4
AUX_BY_PERMUTE = True
NARROW_FAR = False


def shifted_2(value, axis, by):
    count = lax.axis_size(axis)
    return lax.ppermute(value, axis, [(i, (i + by) % count) for i in range(count)])


def general_plan(integrals, occ_energy, vir_energy):
    row_count = integrals.shape[0]
    vir_width = integrals.shape[1]
    cycle_size = lax.axis_size("occ")
    position = lax.axis_index("occ")
    own_level = lax.dynamic_slice_in_dim(occ_energy, position * row_count, row_count)
    partner_level = lax.dynamic_slice_in_dim(
        occ_energy, (position - 2) % cycle_size * row_count, row_count
    )
    local_vir = lax.dynamic_slice_in_dim(vir_energy, lax.axis_index("vir") * vir_width, vir_width)
    shifted = shifted_2(integrals, "occ", 2)
    partner = lax.all_gather(shifted, "vir", axis=1, tiled=True)
    virtuals = partner.shape[1]
    pair_level = own_level + partner_level
    share_rows = virtuals // lax.axis_size("aux")
    partial_value = lax.psum_scatter(
        jnp.einsum("nbq,naq->bna", partner, integrals, preferred_element_type=jnp.float32),
        "aux",
        scatter_dimension=0,
        tiled=True,
    )
    first_row = lax.axis_index("aux") * share_rows
    vir_rows = lax.dynamic_slice_in_dim(vir_energy, first_row, share_rows)
    amplitudes = (
        partial_value
        / (pair_level[None, :, None] - vir_rows[:, None, None] - local_vir[None, None, :])
    ).astype(jnp.bfloat16)
    portion = lax.all_gather(amplitudes, "aux", axis=0, tiled=True)
    own_part = jnp.einsum("bna,nbq->naq", portion, partner, preferred_element_type=jnp.float32)
    rows_back = jnp.einsum("bna,naq->nbq", portion, integrals, preferred_element_type=jnp.float32)
    owned = lax.psum_scatter(rows_back, "vir", scatter_dimension=1, tiled=True)
    returned = shifted_2(owned, "occ", -2)
    return (own_part + returned).astype(jnp.bfloat16)


def xor_pairs(count, step):
    return [(j, j ^ step) for j in range(count)]


def aux_reduce_scatter(x):
    count = lax.axis_size("aux")
    k = lax.axis_index("aux")
    first = 0
    step = 1
    while step < count:
        half = x.shape[0] // 2
        bit = (k // step) % 2
        keep = lax.dynamic_slice_in_dim(x, bit * half, half, 0)
        send = lax.dynamic_slice_in_dim(x, (1 - bit) * half, half, 0)
        if step > 1 and NARROW_FAR:
            x = keep + lax.ppermute(send.astype(jnp.bfloat16), "aux", xor_pairs(count, step))
        else:
            x = keep + lax.ppermute(send, "aux", xor_pairs(count, step))
        first = first + bit * half
        step *= 2
    return x, first


def aux_all_gather(x):
    count = lax.axis_size("aux")
    k = lax.axis_index("aux")
    step = count // 2
    while step >= 1:
        bit = (k // step) % 2
        other = lax.ppermute(x, "aux", xor_pairs(count, step))
        x = jnp.where(bit == 0, jnp.concatenate([x, other]), jnp.concatenate([other, x]))
        step //= 2
    return x


def paired_plan(integrals, occ_energy, vir_energy):
    own = integrals[0]
    vir_rows, _ = own.shape
    cycle_size = lax.axis_size("occ")
    position = lax.axis_index("occ")
    pair_level = occ_energy[position] + occ_energy[(position - 2) % cycle_size]
    vir_pos = lax.axis_index("vir")
    vir_count = lax.axis_size("vir")
    aux_count = lax.axis_size("aux")
    share = vir_rows // aux_count
    width = vir_rows // CHUNKS

    if not AUX_BY_PERMUTE:
        first_row = lax.axis_index("aux") * share

    total = None
    previous = None
    rows_done = None
    partials = []
    for c in range(CHUNKS):
        piece = own[c * width:(c + 1) * width]
        if previous is not None:
            gate = previous
            piece, _ = lax.optimization_barrier((piece, gate))
        arrived = shifted_2(piece, "occ", 2)
        previous = arrived
        if c >= 1:
            arrived, _ = lax.optimization_barrier((arrived, partials[c - 1]))
        if vir_count == 2:
            mate = shifted_2(arrived, "vir", 1)
            block = jnp.concatenate([arrived, mate])
            cols = [vir_pos, 1 - vir_pos]
        else:
            block = lax.all_gather(arrived, "vir", axis=0, tiled=True)
            cols = list(range(vir_count))
        col_level = jnp.concatenate(
            [lax.dynamic_slice_in_dim(vir_energy, w * vir_rows + c * width, width) for w in cols]
        )
        partial = jnp.einsum("aq,bq->ab", own, block, preferred_element_type=jnp.float32)
        partials.append(partial)
        if AUX_BY_PERMUTE:
            summed, first = aux_reduce_scatter(partial)
        else:
            summed = lax.psum_scatter(partial, "aux", scatter_dimension=0, tiled=True)
            first = first_row
        if rows_done is not None:
            summed, _ = lax.optimization_barrier((summed, rows_done))
        row_level = lax.dynamic_slice_in_dim(vir_energy, vir_pos * vir_rows + first, share)
        amplitudes = (summed / (pair_level - row_level[:, None] - col_level[None, :])).astype(
            jnp.bfloat16
        )
        if AUX_BY_PERMUTE:
            rows = aux_all_gather(amplitudes)
        else:
            rows = lax.all_gather(amplitudes, "aux", axis=0, tiled=True)
        rows_done = rows
        term = jnp.dot(rows, block, preferred_element_type=jnp.float32)
        total = term if total is None else total + term
    gamma_own = total
    gamma_back = total
    return (gamma_own + gamma_back).astype(jnp.bfloat16)[None]


def on_device(integrals, occ_energy, vir_energy):
    cycle_size = lax.axis_size("occ")
    if integrals.shape[0] == 1 and 4 % cycle_size == 0 and integrals.shape[1] % (CHUNKS * 8) == 0:
        return paired_plan(integrals, occ_energy, vir_energy)
    return general_plan(integrals, occ_energy, vir_energy)


def solution(mesh):
    placed = (P("occ", "vir", "aux"), P(), P())
    return jax.shard_map(
        on_device, mesh=mesh, in_specs=placed, out_specs=P("occ", "vir", "aux"), check_vma=False
    )
```

```python
import jax
import jax.numpy as jnp
from jax import lax
from jax.sharding import PartitionSpec as P

CHUNKS = 4
AUX_BY_PERMUTE = True
NARROW_FAR = False


def shifted_2(value, axis, by):
    count = lax.axis_size(axis)
    return lax.ppermute(value, axis, [(i, (i + by) % count) for i in range(count)])


def general_plan(integrals, occ_energy, vir_energy):
    row_count = integrals.shape[0]
    vir_width = integrals.shape[1]
    cycle_size = lax.axis_size("occ")
    position = lax.axis_index("occ")
    own_level = lax.dynamic_slice_in_dim(occ_energy, position * row_count, row_count)
    partner_level = lax.dynamic_slice_in_dim(
        occ_energy, (position - 2) % cycle_size * row_count, row_count
    )
    local_vir = lax.dynamic_slice_in_dim(vir_energy, lax.axis_index("vir") * vir_width, vir_width)
    shifted = shifted_2(integrals, "occ", 2)
    partner = lax.all_gather(shifted, "vir", axis=1, tiled=True)
    virtuals = partner.shape[1]
    pair_level = own_level + partner_level
    share_rows = virtuals // lax.axis_size("aux")
    partial_value = lax.psum_scatter(
        jnp.einsum("nbq,naq->bna", partner, integrals, preferred_element_type=jnp.float32),
        "aux",
        scatter_dimension=0,
        tiled=True,
    )
    first_row = lax.axis_index("aux") * share_rows
    vir_rows = lax.dynamic_slice_in_dim(vir_energy, first_row, share_rows)
    amplitudes = (
        partial_value
        / (pair_level[None, :, None] - vir_rows[:, None, None] - local_vir[None, None, :])
    ).astype(jnp.bfloat16)
    portion = lax.all_gather(amplitudes, "aux", axis=0, tiled=True)
    own_part = jnp.einsum("bna,nbq->naq", portion, partner, preferred_element_type=jnp.float32)
    rows_back = jnp.einsum("bna,naq->nbq", portion, integrals, preferred_element_type=jnp.float32)
    owned = lax.psum_scatter(rows_back, "vir", scatter_dimension=1, tiled=True)
    returned = shifted_2(owned, "occ", -2)
    return (own_part + returned).astype(jnp.bfloat16)


def xor_pairs(count, step):
    return [(j, j ^ step) for j in range(count)]


def aux_reduce_scatter(x):
    count = lax.axis_size("aux")
    k = lax.axis_index("aux")
    first = 0
    step = 1
    while step < count:
        half = x.shape[0] // 2
        bit = (k // step) % 2
        keep = lax.dynamic_slice_in_dim(x, bit * half, half, 0)
        send = lax.dynamic_slice_in_dim(x, (1 - bit) * half, half, 0)
        if step > 1 and NARROW_FAR:
            x = keep + lax.ppermute(send.astype(jnp.bfloat16), "aux", xor_pairs(count, step))
        else:
            x = keep + lax.ppermute(send, "aux", xor_pairs(count, step))
        first = first + bit * half
        step *= 2
    return x, first


def aux_all_gather(x):
    count = lax.axis_size("aux")
    k = lax.axis_index("aux")
    step = count // 2
    while step >= 1:
        bit = (k // step) % 2
        other = lax.ppermute(x, "aux", xor_pairs(count, step))
        x = jnp.where(bit == 0, jnp.concatenate([x, other]), jnp.concatenate([other, x]))
        step //= 2
    return x


def paired_plan(integrals, occ_energy, vir_energy):
    own = integrals[0]
    vir_rows, _ = own.shape
    cycle_size = lax.axis_size("occ")
    position = lax.axis_index("occ")
    pair_level = occ_energy[position] + occ_energy[(position - 2) % cycle_size]
    vir_pos = lax.axis_index("vir")
    vir_count = lax.axis_size("vir")
    aux_count = lax.axis_size("aux")
    share = vir_rows // aux_count
    width = vir_rows // CHUNKS

    if not AUX_BY_PERMUTE:
        first_row = lax.axis_index("aux") * share

    total = None
    previous = None
    rows_done = None
    for c in range(CHUNKS):
        source = own
        if previous is not None:
            source, _ = lax.optimization_barrier((own, previous))
        piece = source[c * width:(c + 1) * width]
        arrived = shifted_2(piece, "occ", 2)
        previous = arrived
        if vir_count == 2:
            mate = shifted_2(arrived, "vir", 1)
            block = jnp.concatenate([arrived, mate])
            cols = [vir_pos, 1 - vir_pos]
        else:
            block = lax.all_gather(arrived, "vir", axis=0, tiled=True)
            cols = list(range(vir_count))
        col_level = jnp.concatenate(
            [lax.dynamic_slice_in_dim(vir_energy, w * vir_rows + c * width, width) for w in cols]
        )
        partial = jnp.einsum("aq,bq->ab", own, block, preferred_element_type=jnp.float32)
        if AUX_BY_PERMUTE:
            summed, first = aux_reduce_scatter(partial)
        else:
            summed = lax.psum_scatter(partial, "aux", scatter_dimension=0, tiled=True)
            first = first_row
        if rows_done is not None:
            summed, _ = lax.optimization_barrier((summed, rows_done))
        row_level = lax.dynamic_slice_in_dim(vir_energy, vir_pos * vir_rows + first, share)
        amplitudes = (summed / (pair_level - row_level[:, None] - col_level[None, :])).astype(
            jnp.bfloat16
        )
        if AUX_BY_PERMUTE:
            rows = aux_all_gather(amplitudes)
        else:
            rows = lax.all_gather(amplitudes, "aux", axis=0, tiled=True)
        rows_done = rows
        term = jnp.dot(rows, block, preferred_element_type=jnp.float32)
        total = term if total is None else total + term
    gamma_own = total
    gamma_back = total
    return (gamma_own + gamma_back).astype(jnp.bfloat16)[None]


def on_device(integrals, occ_energy, vir_energy):
    cycle_size = lax.axis_size("occ")
    if integrals.shape[0] == 1 and 4 % cycle_size == 0 and integrals.shape[1] % (CHUNKS * 8) == 0:
        return paired_plan(integrals, occ_energy, vir_energy)
    return general_plan(integrals, occ_energy, vir_energy)


def solution(mesh):
    placed = (P("occ", "vir", "aux"), P(), P())
    return jax.shard_map(
        on_device, mesh=mesh, in_specs=placed, out_specs=P("occ", "vir", "aux"), check_vma=False
    )
```

```python
import jax
import jax.numpy as jnp
from jax import lax
from jax.sharding import PartitionSpec as P

CHUNKS = 4
AUX_BY_PERMUTE = True
NARROW_FAR = False


def shifted_2(value, axis, by):
    count = lax.axis_size(axis)
    return lax.ppermute(value, axis, [(i, (i + by) % count) for i in range(count)])


def general_plan(integrals, occ_energy, vir_energy):
    row_count = integrals.shape[0]
    vir_width = integrals.shape[1]
    cycle_size = lax.axis_size("occ")
    position = lax.axis_index("occ")
    own_level = lax.dynamic_slice_in_dim(occ_energy, position * row_count, row_count)
    partner_level = lax.dynamic_slice_in_dim(
        occ_energy, (position - 2) % cycle_size * row_count, row_count
    )
    local_vir = lax.dynamic_slice_in_dim(vir_energy, lax.axis_index("vir") * vir_width, vir_width)
    shifted = shifted_2(integrals, "occ", 2)
    partner = lax.all_gather(shifted, "vir", axis=1, tiled=True)
    virtuals = partner.shape[1]
    pair_level = own_level + partner_level
    share_rows = virtuals // lax.axis_size("aux")
    partial_value = lax.psum_scatter(
        jnp.einsum("nbq,naq->bna", partner, integrals, preferred_element_type=jnp.float32),
        "aux",
        scatter_dimension=0,
        tiled=True,
    )
    first_row = lax.axis_index("aux") * share_rows
    vir_rows = lax.dynamic_slice_in_dim(vir_energy, first_row, share_rows)
    amplitudes = (
        partial_value
        / (pair_level[None, :, None] - vir_rows[:, None, None] - local_vir[None, None, :])
    ).astype(jnp.bfloat16)
    portion = lax.all_gather(amplitudes, "aux", axis=0, tiled=True)
    own_part = jnp.einsum("bna,nbq->naq", portion, partner, preferred_element_type=jnp.float32)
    rows_back = jnp.einsum("bna,naq->nbq", portion, integrals, preferred_element_type=jnp.float32)
    owned = lax.psum_scatter(rows_back, "vir", scatter_dimension=1, tiled=True)
    returned = shifted_2(owned, "occ", -2)
    return (own_part + returned).astype(jnp.bfloat16)


def xor_pairs(count, step):
    return [(j, j ^ step) for j in range(count)]


def aux_reduce_scatter(x, first=0, step=1, stop=None):
    count = lax.axis_size("aux")
    k = lax.axis_index("aux")
    stop = count if stop is None else stop
    while step < stop:
        half = x.shape[0] // 2
        bit = (k // step) % 2
        keep = lax.dynamic_slice_in_dim(x, bit * half, half, 0)
        send = lax.dynamic_slice_in_dim(x, (1 - bit) * half, half, 0)
        if step > 1 and NARROW_FAR:
            x = keep + lax.ppermute(send.astype(jnp.bfloat16), "aux", xor_pairs(count, step))
        else:
            x = keep + lax.ppermute(send, "aux", xor_pairs(count, step))
        first = first + bit * half
        step *= 2
    return x, first


def aux_all_gather(x):
    count = lax.axis_size("aux")
    k = lax.axis_index("aux")
    step = count // 2
    while step >= 1:
        bit = (k // step) % 2
        other = lax.ppermute(x, "aux", xor_pairs(count, step))
        x = jnp.where(bit == 0, jnp.concatenate([x, other]), jnp.concatenate([other, x]))
        step //= 2
    return x


def paired_plan(integrals, occ_energy, vir_energy):
    own = integrals[0]
    vir_rows, _ = own.shape
    cycle_size = lax.axis_size("occ")
    position = lax.axis_index("occ")
    pair_level = occ_energy[position] + occ_energy[(position - 2) % cycle_size]
    vir_pos = lax.axis_index("vir")
    vir_count = lax.axis_size("vir")
    aux_count = lax.axis_size("aux")
    share = vir_rows // aux_count
    width = vir_rows // CHUNKS

    if not AUX_BY_PERMUTE:
        first_row = lax.axis_index("aux") * share

    total = None
    previous = None
    rows_done = None
    near = []
    for c in range(CHUNKS):
        piece = own[c * width:(c + 1) * width]
        if previous is not None:
            piece, _ = lax.optimization_barrier((piece, previous))
        arrived = shifted_2(piece, "occ", 2)
        previous = arrived
        if c >= 2:
            arrived, _ = lax.optimization_barrier((arrived, near[c - 2]))
        if vir_count == 2:
            mate = shifted_2(arrived, "vir", 1)
            block = jnp.concatenate([arrived, mate])
            cols = [vir_pos, 1 - vir_pos]
        else:
            block = lax.all_gather(arrived, "vir", axis=0, tiled=True)
            cols = list(range(vir_count))
        col_level = jnp.concatenate(
            [lax.dynamic_slice_in_dim(vir_energy, w * vir_rows + c * width, width) for w in cols]
        )
        partial = jnp.einsum("aq,bq->ab", own, block, preferred_element_type=jnp.float32)
        if AUX_BY_PERMUTE:
            summed, first = aux_reduce_scatter(partial, stop=2)
            near.append(summed)
            summed, first = aux_reduce_scatter(summed, first, step=2)
        else:
            summed = lax.psum_scatter(partial, "aux", scatter_dimension=0, tiled=True)
            first = first_row
        if rows_done is not None:
            summed, _ = lax.optimization_barrier((summed, rows_done))
        row_level = lax.dynamic_slice_in_dim(vir_energy, vir_pos * vir_rows + first, share)
        amplitudes = (summed / (pair_level - row_level[:, None] - col_level[None, :])).astype(
            jnp.bfloat16
        )
        if AUX_BY_PERMUTE:
            rows = aux_all_gather(amplitudes)
        else:
            rows = lax.all_gather(amplitudes, "aux", axis=0, tiled=True)
        rows_done = rows
        term = jnp.dot(rows, block, preferred_element_type=jnp.float32)
        total = term if total is None else total + term
    gamma_own = total
    gamma_back = total
    return (gamma_own + gamma_back).astype(jnp.bfloat16)[None]


def on_device(integrals, occ_energy, vir_energy):
    cycle_size = lax.axis_size("occ")
    if integrals.shape[0] == 1 and 4 % cycle_size == 0 and integrals.shape[1] % (CHUNKS * 8) == 0:
        return paired_plan(integrals, occ_energy, vir_energy)
    return general_plan(integrals, occ_energy, vir_energy)


def solution(mesh):
    placed = (P("occ", "vir", "aux"), P(), P())
    return jax.shard_map(
        on_device, mesh=mesh, in_specs=placed, out_specs=P("occ", "vir", "aux"), check_vma=False
    )
```

```python
import jax
import jax.numpy as jnp
from jax import lax
from jax.sharding import PartitionSpec as P

CHUNKS = 4
AUX_BY_PERMUTE = True
NARROW_FAR = False


def shifted_2(value, axis, by):
    count = lax.axis_size(axis)
    return lax.ppermute(value, axis, [(i, (i + by) % count) for i in range(count)])


def general_plan(integrals, occ_energy, vir_energy):
    row_count = integrals.shape[0]
    vir_width = integrals.shape[1]
    cycle_size = lax.axis_size("occ")
    position = lax.axis_index("occ")
    own_level = lax.dynamic_slice_in_dim(occ_energy, position * row_count, row_count)
    partner_level = lax.dynamic_slice_in_dim(
        occ_energy, (position - 2) % cycle_size * row_count, row_count
    )
    local_vir = lax.dynamic_slice_in_dim(vir_energy, lax.axis_index("vir") * vir_width, vir_width)
    shifted = shifted_2(integrals, "occ", 2)
    partner = lax.all_gather(shifted, "vir", axis=1, tiled=True)
    virtuals = partner.shape[1]
    pair_level = own_level + partner_level
    share_rows = virtuals // lax.axis_size("aux")
    partial_value = lax.psum_scatter(
        jnp.einsum("nbq,naq->bna", partner, integrals, preferred_element_type=jnp.float32),
        "aux",
        scatter_dimension=0,
        tiled=True,
    )
    first_row = lax.axis_index("aux") * share_rows
    vir_rows = lax.dynamic_slice_in_dim(vir_energy, first_row, share_rows)
    amplitudes = (
        partial_value
        / (pair_level[None, :, None] - vir_rows[:, None, None] - local_vir[None, None, :])
    ).astype(jnp.bfloat16)
    portion = lax.all_gather(amplitudes, "aux", axis=0, tiled=True)
    own_part = jnp.einsum("bna,nbq->naq", portion, partner, preferred_element_type=jnp.float32)
    rows_back = jnp.einsum("bna,naq->nbq", portion, integrals, preferred_element_type=jnp.float32)
    owned = lax.psum_scatter(rows_back, "vir", scatter_dimension=1, tiled=True)
    returned = shifted_2(owned, "occ", -2)
    return (own_part + returned).astype(jnp.bfloat16)


def xor_pairs(count, step):
    return [(j, j ^ step) for j in range(count)]


def aux_reduce_scatter(x):
    count = lax.axis_size("aux")
    k = lax.axis_index("aux")
    first = 0
    step = 1
    while step < count:
        half = x.shape[0] // 2
        bit = (k // step) % 2
        keep = lax.dynamic_slice_in_dim(x, bit * half, half, 0)
        send = lax.dynamic_slice_in_dim(x, (1 - bit) * half, half, 0)
        if step > 1 and NARROW_FAR:
            x = keep + lax.ppermute(send.astype(jnp.bfloat16), "aux", xor_pairs(count, step))
        else:
            x = keep + lax.ppermute(send, "aux", xor_pairs(count, step))
        first = first + bit * half
        step *= 2
    return x, first


def aux_all_gather(x):
    count = lax.axis_size("aux")
    k = lax.axis_index("aux")
    step = count // 2
    while step >= 1:
        bit = (k // step) % 2
        other = lax.ppermute(x, "aux", xor_pairs(count, step))
        x = jnp.where(bit == 0, jnp.concatenate([x, other]), jnp.concatenate([other, x]))
        step //= 2
    return x


def paired_plan(integrals, occ_energy, vir_energy):
    own = integrals[0]
    vir_rows, _ = own.shape
    cycle_size = lax.axis_size("occ")
    position = lax.axis_index("occ")
    pair_level = occ_energy[position] + occ_energy[(position - 2) % cycle_size]
    vir_pos = lax.axis_index("vir")
    vir_count = lax.axis_size("vir")
    aux_count = lax.axis_size("aux")
    share = vir_rows // aux_count
    width = vir_rows // CHUNKS

    if not AUX_BY_PERMUTE:
        first_row = lax.axis_index("aux") * share

    total = None
    previous = None
    rows_done = None
    for c in range(CHUNKS):
        piece = own[c * width:(c + 1) * width]
        if previous is not None:
            piece, _ = lax.optimization_barrier((piece, previous))
        arrived = shifted_2(piece, "occ", 2)
        previous = arrived
        if vir_count == 2:
            mate = shifted_2(arrived, "vir", 1)
            block = jnp.concatenate([arrived, mate])
            cols = [vir_pos, 1 - vir_pos]
        else:
            block = lax.all_gather(arrived, "vir", axis=0, tiled=True)
            cols = list(range(vir_count))
        col_level = jnp.concatenate(
            [lax.dynamic_slice_in_dim(vir_energy, w * vir_rows + c * width, width) for w in cols]
        )
        partial = jnp.einsum("aq,bq->ab", own, block, preferred_element_type=jnp.float32)
        if AUX_BY_PERMUTE:
            summed, first = aux_reduce_scatter(partial)
        else:
            summed = lax.psum_scatter(partial, "aux", scatter_dimension=0, tiled=True)
            first = first_row
        if rows_done is not None:
            summed, _ = lax.optimization_barrier((summed, rows_done))
        row_level = lax.dynamic_slice_in_dim(vir_energy, vir_pos * vir_rows + first, share)
        amplitudes = (summed / (pair_level - row_level[:, None] - col_level[None, :])).astype(
            jnp.bfloat16
        )
        if AUX_BY_PERMUTE:
            rows = aux_all_gather(amplitudes)
        else:
            rows = lax.all_gather(amplitudes, "aux", axis=0, tiled=True)
        rows_done = amplitudes
        term = jnp.dot(rows, block, preferred_element_type=jnp.float32)
        total = term if total is None else total + term
    gamma_own = total
    gamma_back = total
    return (gamma_own + gamma_back).astype(jnp.bfloat16)[None]


def on_device(integrals, occ_energy, vir_energy):
    cycle_size = lax.axis_size("occ")
    if integrals.shape[0] == 1 and 4 % cycle_size == 0 and integrals.shape[1] % (CHUNKS * 8) == 0:
        return paired_plan(integrals, occ_energy, vir_energy)
    return general_plan(integrals, occ_energy, vir_energy)


def solution(mesh):
    placed = (P("occ", "vir", "aux"), P(), P())
    return jax.shard_map(
        on_device, mesh=mesh, in_specs=placed, out_specs=P("occ", "vir", "aux"), check_vma=False
    )
```

```python
import jax
import jax.numpy as jnp
from jax import lax
from jax.sharding import PartitionSpec as P

WIDTHS = (128, 128, 256, 256, 256)
AUX_BY_PERMUTE = True
NARROW_FAR = False


def shifted_2(value, axis, by):
    count = lax.axis_size(axis)
    return lax.ppermute(value, axis, [(i, (i + by) % count) for i in range(count)])


def general_plan(integrals, occ_energy, vir_energy):
    row_count = integrals.shape[0]
    vir_width = integrals.shape[1]
    cycle_size = lax.axis_size("occ")
    position = lax.axis_index("occ")
    own_level = lax.dynamic_slice_in_dim(occ_energy, position * row_count, row_count)
    partner_level = lax.dynamic_slice_in_dim(
        occ_energy, (position - 2) % cycle_size * row_count, row_count
    )
    local_vir = lax.dynamic_slice_in_dim(vir_energy, lax.axis_index("vir") * vir_width, vir_width)
    shifted = shifted_2(integrals, "occ", 2)
    partner = lax.all_gather(shifted, "vir", axis=1, tiled=True)
    virtuals = partner.shape[1]
    pair_level = own_level + partner_level
    share_rows = virtuals // lax.axis_size("aux")
    partial_value = lax.psum_scatter(
        jnp.einsum("nbq,naq->bna", partner, integrals, preferred_element_type=jnp.float32),
        "aux",
        scatter_dimension=0,
        tiled=True,
    )
    first_row = lax.axis_index("aux") * share_rows
    vir_rows = lax.dynamic_slice_in_dim(vir_energy, first_row, share_rows)
    amplitudes = (
        partial_value
        / (pair_level[None, :, None] - vir_rows[:, None, None] - local_vir[None, None, :])
    ).astype(jnp.bfloat16)
    portion = lax.all_gather(amplitudes, "aux", axis=0, tiled=True)
    own_part = jnp.einsum("bna,nbq->naq", portion, partner, preferred_element_type=jnp.float32)
    rows_back = jnp.einsum("bna,naq->nbq", portion, integrals, preferred_element_type=jnp.float32)
    owned = lax.psum_scatter(rows_back, "vir", scatter_dimension=1, tiled=True)
    returned = shifted_2(owned, "occ", -2)
    return (own_part + returned).astype(jnp.bfloat16)


def xor_pairs(count, step):
    return [(j, j ^ step) for j in range(count)]


def aux_reduce_scatter(x):
    count = lax.axis_size("aux")
    k = lax.axis_index("aux")
    first = 0
    step = 1
    while step < count:
        half = x.shape[0] // 2
        bit = (k // step) % 2
        keep = lax.dynamic_slice_in_dim(x, bit * half, half, 0)
        send = lax.dynamic_slice_in_dim(x, (1 - bit) * half, half, 0)
        if step > 1 and NARROW_FAR:
            x = keep + lax.ppermute(send.astype(jnp.bfloat16), "aux", xor_pairs(count, step))
        else:
            x = keep + lax.ppermute(send, "aux", xor_pairs(count, step))
        first = first + bit * half
        step *= 2
    return x, first


def aux_all_gather(x):
    count = lax.axis_size("aux")
    k = lax.axis_index("aux")
    step = count // 2
    while step >= 1:
        bit = (k // step) % 2
        other = lax.ppermute(x, "aux", xor_pairs(count, step))
        x = jnp.where(bit == 0, jnp.concatenate([x, other]), jnp.concatenate([other, x]))
        step //= 2
    return x


def paired_plan(integrals, occ_energy, vir_energy):
    own = integrals[0]
    vir_rows, _ = own.shape
    cycle_size = lax.axis_size("occ")
    position = lax.axis_index("occ")
    pair_level = occ_energy[position] + occ_energy[(position - 2) % cycle_size]
    vir_pos = lax.axis_index("vir")
    vir_count = lax.axis_size("vir")
    aux_count = lax.axis_size("aux")
    share = vir_rows // aux_count
    widths = [w * (vir_rows // sum(WIDTHS)) for w in WIDTHS]
    starts = [sum(widths[:c]) for c in range(len(widths))]

    if not AUX_BY_PERMUTE:
        first_row = lax.axis_index("aux") * share

    total = None
    previous = None
    rows_done = None
    for c, width in enumerate(widths):
        piece = own[starts[c]:starts[c] + width]
        if previous is not None:
            piece, _ = lax.optimization_barrier((piece, previous))
        arrived = shifted_2(piece, "occ", 2)
        previous = arrived
        if vir_count == 2:
            mate = shifted_2(arrived, "vir", 1)
            block = jnp.concatenate([arrived, mate])
            cols = [vir_pos, 1 - vir_pos]
        else:
            block = lax.all_gather(arrived, "vir", axis=0, tiled=True)
            cols = list(range(vir_count))
        col_level = jnp.concatenate(
            [lax.dynamic_slice_in_dim(vir_energy, w * vir_rows + starts[c], width) for w in cols]
        )
        partial = jnp.einsum("aq,bq->ab", own, block, preferred_element_type=jnp.float32)
        if AUX_BY_PERMUTE:
            summed, first = aux_reduce_scatter(partial)
        else:
            summed = lax.psum_scatter(partial, "aux", scatter_dimension=0, tiled=True)
            first = first_row
        if rows_done is not None:
            summed, _ = lax.optimization_barrier((summed, rows_done))
        row_level = lax.dynamic_slice_in_dim(vir_energy, vir_pos * vir_rows + first, share)
        amplitudes = (summed / (pair_level - row_level[:, None] - col_level[None, :])).astype(
            jnp.bfloat16
        )
        if AUX_BY_PERMUTE:
            rows = aux_all_gather(amplitudes)
        else:
            rows = lax.all_gather(amplitudes, "aux", axis=0, tiled=True)
        rows_done = rows
        term = jnp.dot(rows, block, preferred_element_type=jnp.float32)
        total = term if total is None else total + term
    gamma_own = total
    gamma_back = total
    return (gamma_own + gamma_back).astype(jnp.bfloat16)[None]


def on_device(integrals, occ_energy, vir_energy):
    cycle_size = lax.axis_size("occ")
    if integrals.shape[0] == 1 and 4 % cycle_size == 0 and integrals.shape[1] % sum(WIDTHS) == 0:
        return paired_plan(integrals, occ_energy, vir_energy)
    return general_plan(integrals, occ_energy, vir_energy)


def solution(mesh):
    placed = (P("occ", "vir", "aux"), P(), P())
    return jax.shard_map(
        on_device, mesh=mesh, in_specs=placed, out_specs=P("occ", "vir", "aux"), check_vma=False
    )
```

```python
import jax
import jax.numpy as jnp
from jax import lax
from jax.sharding import Mesh, PartitionSpec as P

CHUNKS = 4
AUX_BY_PERMUTE = True
NARROW_FAR = False
SPLIT_OCC = True


def shifted_2(value, axis, by):
    count = lax.axis_size(axis)
    return lax.ppermute(value, axis, [(i, (i + by) % count) for i in range(count)])


def general_plan(integrals, occ_energy, vir_energy):
    row_count = integrals.shape[0]
    vir_width = integrals.shape[1]
    cycle_size = lax.axis_size("occ")
    position = lax.axis_index("occ")
    own_level = lax.dynamic_slice_in_dim(occ_energy, position * row_count, row_count)
    partner_level = lax.dynamic_slice_in_dim(
        occ_energy, (position - 2) % cycle_size * row_count, row_count
    )
    local_vir = lax.dynamic_slice_in_dim(vir_energy, lax.axis_index("vir") * vir_width, vir_width)
    shifted = shifted_2(integrals, "occ", 2)
    partner = lax.all_gather(shifted, "vir", axis=1, tiled=True)
    virtuals = partner.shape[1]
    pair_level = own_level + partner_level
    share_rows = virtuals // lax.axis_size("aux")
    partial_value = lax.psum_scatter(
        jnp.einsum("nbq,naq->bna", partner, integrals, preferred_element_type=jnp.float32),
        "aux",
        scatter_dimension=0,
        tiled=True,
    )
    first_row = lax.axis_index("aux") * share_rows
    vir_rows = lax.dynamic_slice_in_dim(vir_energy, first_row, share_rows)
    amplitudes = (
        partial_value
        / (pair_level[None, :, None] - vir_rows[:, None, None] - local_vir[None, None, :])
    ).astype(jnp.bfloat16)
    portion = lax.all_gather(amplitudes, "aux", axis=0, tiled=True)
    own_part = jnp.einsum("bna,nbq->naq", portion, partner, preferred_element_type=jnp.float32)
    rows_back = jnp.einsum("bna,naq->nbq", portion, integrals, preferred_element_type=jnp.float32)
    owned = lax.psum_scatter(rows_back, "vir", scatter_dimension=1, tiled=True)
    returned = shifted_2(owned, "occ", -2)
    return (own_part + returned).astype(jnp.bfloat16)


def xor_pairs(count, step):
    return [(j, j ^ step) for j in range(count)]


def aux_reduce_scatter(x):
    count = lax.axis_size("aux")
    k = lax.axis_index("aux")
    first = 0
    step = 1
    while step < count:
        half = x.shape[0] // 2
        bit = (k // step) % 2
        keep = lax.dynamic_slice_in_dim(x, bit * half, half, 0)
        send = lax.dynamic_slice_in_dim(x, (1 - bit) * half, half, 0)
        if step > 1 and NARROW_FAR:
            x = keep + lax.ppermute(send.astype(jnp.bfloat16), "aux", xor_pairs(count, step))
        else:
            x = keep + lax.ppermute(send, "aux", xor_pairs(count, step))
        first = first + bit * half
        step *= 2
    return x, first


def aux_all_gather(x):
    count = lax.axis_size("aux")
    k = lax.axis_index("aux")
    step = count // 2
    while step >= 1:
        bit = (k // step) % 2
        other = lax.ppermute(x, "aux", xor_pairs(count, step))
        x = jnp.where(bit == 0, jnp.concatenate([x, other]), jnp.concatenate([other, x]))
        step //= 2
    return x


def paired_plan(integrals, occ_energy, vir_energy, occ="occ", swap=False):
    own = integrals[0]
    vir_rows, _ = own.shape
    cycle_size = lax.axis_size(occ)
    position = lax.axis_index(occ)
    pair_level = occ_energy[position] + occ_energy[(position - 2) % cycle_size]
    vir_pos = lax.axis_index("vir")
    vir_count = lax.axis_size("vir")
    aux_count = lax.axis_size("aux")
    share = vir_rows // aux_count
    width = vir_rows // CHUNKS

    if not AUX_BY_PERMUTE:
        first_row = lax.axis_index("aux") * share

    total = None
    previous = None
    rows_done = None
    for c in range(CHUNKS):
        piece = own[c * width:(c + 1) * width]
        if previous is not None:
            piece, _ = lax.optimization_barrier((piece, previous))
        if swap:
            both = lax.all_to_all(jnp.stack([piece, piece]), "occ_hi", 0, 0)
            arrived = lax.dynamic_index_in_dim(both, 1 - lax.axis_index("occ_hi"), 0, False)
        else:
            arrived = shifted_2(piece, "occ", 2)
        previous = arrived
        if vir_count == 2:
            mate = shifted_2(arrived, "vir", 1)
            block = jnp.concatenate([arrived, mate])
            cols = [vir_pos, 1 - vir_pos]
        else:
            block = lax.all_gather(arrived, "vir", axis=0, tiled=True)
            cols = list(range(vir_count))
        col_level = jnp.concatenate(
            [lax.dynamic_slice_in_dim(vir_energy, w * vir_rows + c * width, width) for w in cols]
        )
        partial = jnp.einsum("aq,bq->ab", own, block, preferred_element_type=jnp.float32)
        if AUX_BY_PERMUTE:
            summed, first = aux_reduce_scatter(partial)
        else:
            summed = lax.psum_scatter(partial, "aux", scatter_dimension=0, tiled=True)
            first = first_row
        if rows_done is not None:
            summed, _ = lax.optimization_barrier((summed, rows_done))
        row_level = lax.dynamic_slice_in_dim(vir_energy, vir_pos * vir_rows + first, share)
        amplitudes = (summed / (pair_level - row_level[:, None] - col_level[None, :])).astype(
            jnp.bfloat16
        )
        if AUX_BY_PERMUTE:
            rows = aux_all_gather(amplitudes)
        else:
            rows = lax.all_gather(amplitudes, "aux", axis=0, tiled=True)
        rows_done = rows
        term = jnp.dot(rows, block, preferred_element_type=jnp.float32)
        total = term if total is None else total + term
    gamma_own = total
    gamma_back = total
    return (gamma_own + gamma_back).astype(jnp.bfloat16)[None]


def on_device(integrals, occ_energy, vir_energy):
    cycle_size = lax.axis_size("occ")
    if integrals.shape[0] == 1 and 4 % cycle_size == 0 and integrals.shape[1] % (CHUNKS * 8) == 0:
        return paired_plan(integrals, occ_energy, vir_energy)
    return general_plan(integrals, occ_energy, vir_energy)


def paired_on_split(integrals, occ_energy, vir_energy):
    return paired_plan(integrals, occ_energy, vir_energy, ("occ_hi", "occ_lo"), True)


def solution(mesh):
    if mesh.shape["occ"] == 4 and mesh.devices.shape[1] % 4 == 0 and SPLIT_OCC:
        names = list(mesh.axis_names)
        at = names.index("occ")
        shape = mesh.devices.shape
        split = Mesh(
            mesh.devices.reshape(shape[:at] + (2, 2) + shape[at + 1:]),
            tuple(names[:at] + ["occ_hi", "occ_lo"] + names[at + 1:]),
        )
        spec = P(("occ_hi", "occ_lo"), "vir", "aux")
        return jax.shard_map(
            paired_on_split, mesh=split, in_specs=(spec, P(), P()), out_specs=spec,
            check_vma=False,
        )
    placed = (P("occ", "vir", "aux"), P(), P())
    return jax.shard_map(
        on_device, mesh=mesh, in_specs=placed, out_specs=P("occ", "vir", "aux"), check_vma=False
    )
```

```python
import jax
import jax.numpy as jnp
from jax import lax
from jax.sharding import PartitionSpec as P

CHUNKS = 4
AUX_BY_PERMUTE = True
NARROW_FAR = False


def shifted_2(value, axis, by):
    count = lax.axis_size(axis)
    return lax.ppermute(value, axis, [(i, (i + by) % count) for i in range(count)])


def general_plan(integrals, occ_energy, vir_energy):
    row_count = integrals.shape[0]
    vir_width = integrals.shape[1]
    cycle_size = lax.axis_size("occ")
    position = lax.axis_index("occ")
    own_level = lax.dynamic_slice_in_dim(occ_energy, position * row_count, row_count)
    partner_level = lax.dynamic_slice_in_dim(
        occ_energy, (position - 2) % cycle_size * row_count, row_count
    )
    local_vir = lax.dynamic_slice_in_dim(vir_energy, lax.axis_index("vir") * vir_width, vir_width)
    shifted = shifted_2(integrals, "occ", 2)
    partner = lax.all_gather(shifted, "vir", axis=1, tiled=True)
    virtuals = partner.shape[1]
    pair_level = own_level + partner_level
    share_rows = virtuals // lax.axis_size("aux")
    partial_value = lax.psum_scatter(
        jnp.einsum("nbq,naq->bna", partner, integrals, preferred_element_type=jnp.float32),
        "aux",
        scatter_dimension=0,
        tiled=True,
    )
    first_row = lax.axis_index("aux") * share_rows
    vir_rows = lax.dynamic_slice_in_dim(vir_energy, first_row, share_rows)
    amplitudes = (
        partial_value
        / (pair_level[None, :, None] - vir_rows[:, None, None] - local_vir[None, None, :])
    ).astype(jnp.bfloat16)
    portion = lax.all_gather(amplitudes, "aux", axis=0, tiled=True)
    own_part = jnp.einsum("bna,nbq->naq", portion, partner, preferred_element_type=jnp.float32)
    rows_back = jnp.einsum("bna,naq->nbq", portion, integrals, preferred_element_type=jnp.float32)
    owned = lax.psum_scatter(rows_back, "vir", scatter_dimension=1, tiled=True)
    returned = shifted_2(owned, "occ", -2)
    return (own_part + returned).astype(jnp.bfloat16)


def xor_pairs(count, step):
    return [(j, j ^ step) for j in range(count)]


def aux_reduce_scatter(x):
    count = lax.axis_size("aux")
    k = lax.axis_index("aux")
    first = 0
    step = 1
    while step < count:
        half = x.shape[0] // 2
        bit = (k // step) % 2
        keep = lax.dynamic_slice_in_dim(x, bit * half, half, 0)
        send = lax.dynamic_slice_in_dim(x, (1 - bit) * half, half, 0)
        if step > 1 and NARROW_FAR:
            x = keep + lax.ppermute(send.astype(jnp.bfloat16), "aux", xor_pairs(count, step))
        else:
            x = keep + lax.ppermute(send, "aux", xor_pairs(count, step))
        first = first + bit * half
        step *= 2
    return x, first


def aux_all_gather(x):
    count = lax.axis_size("aux")
    k = lax.axis_index("aux")
    step = count // 2
    while step >= 1:
        bit = (k // step) % 2
        other = lax.ppermute(x, "aux", xor_pairs(count, step))
        x = jnp.where(bit == 0, jnp.concatenate([x, other]), jnp.concatenate([other, x]))
        step //= 2
    return x


def paired_plan(integrals, occ_energy, vir_energy):
    own = integrals[0]
    vir_rows, _ = own.shape
    cycle_size = lax.axis_size("occ")
    position = lax.axis_index("occ")
    pair_level = occ_energy[position] + occ_energy[(position - 2) % cycle_size]
    vir_pos = lax.axis_index("vir")
    vir_count = lax.axis_size("vir")
    aux_count = lax.axis_size("aux")
    share = vir_rows // aux_count
    width = vir_rows // CHUNKS

    total = None
    previous = None
    rows_done = None
    mate = None
    for t in range(CHUNKS + 1):
        parts, levels = [], []
        if t < CHUNKS:
            piece = own[t * width:(t + 1) * width]
            if previous is not None:
                piece, _ = lax.optimization_barrier((piece, previous))
            arrived = shifted_2(piece, "occ", 2)
            previous = arrived
            parts.append(arrived)
            levels.append(lax.dynamic_slice_in_dim(vir_energy, vir_pos * vir_rows + t * width, width))
        if mate is not None:
            parts.append(mate)
            levels.append(
                lax.dynamic_slice_in_dim(vir_energy, (1 - vir_pos) * vir_rows + (t - 1) * width, width)
            )
        mate = shifted_2(arrived, "vir", 1) if t < CHUNKS else None
        block = jnp.concatenate(parts) if len(parts) > 1 else parts[0]
        col_level = jnp.concatenate(levels) if len(levels) > 1 else levels[0]
        partial = jnp.einsum("aq,bq->ab", own, block, preferred_element_type=jnp.float32)
        summed, first = aux_reduce_scatter(partial)
        if rows_done is not None:
            summed, _ = lax.optimization_barrier((summed, rows_done))
        row_level = lax.dynamic_slice_in_dim(vir_energy, vir_pos * vir_rows + first, share)
        amplitudes = (summed / (pair_level - row_level[:, None] - col_level[None, :])).astype(
            jnp.bfloat16
        )
        rows = aux_all_gather(amplitudes)
        rows_done = rows
        term = jnp.dot(rows, block, preferred_element_type=jnp.float32)
        total = term if total is None else total + term
    gamma_own = total
    gamma_back = total
    return (gamma_own + gamma_back).astype(jnp.bfloat16)[None]


def on_device(integrals, occ_energy, vir_energy):
    cycle_size = lax.axis_size("occ")
    pairs_here = integrals.shape[0] == 1 and 4 % cycle_size == 0 and lax.axis_size("vir") == 2
    if pairs_here and integrals.shape[1] % (CHUNKS * 8) == 0:
        return paired_plan(integrals, occ_energy, vir_energy)
    return general_plan(integrals, occ_energy, vir_energy)


def solution(mesh):
    placed = (P("occ", "vir", "aux"), P(), P())
    return jax.shard_map(
        on_device, mesh=mesh, in_specs=placed, out_specs=P("occ", "vir", "aux"), check_vma=False
    )
```

```python
import jax
import jax.numpy as jnp
from jax import lax
from jax.sharding import PartitionSpec as P

CHUNKS = 4
AUX_BY_PERMUTE = True
NARROW_FAR = False


def shifted_2(value, axis, by):
    count = lax.axis_size(axis)
    return lax.ppermute(value, axis, [(i, (i + by) % count) for i in range(count)])


def general_plan(integrals, occ_energy, vir_energy):
    row_count = integrals.shape[0]
    vir_width = integrals.shape[1]
    cycle_size = lax.axis_size("occ")
    position = lax.axis_index("occ")
    own_level = lax.dynamic_slice_in_dim(occ_energy, position * row_count, row_count)
    partner_level = lax.dynamic_slice_in_dim(
        occ_energy, (position - 2) % cycle_size * row_count, row_count
    )
    local_vir = lax.dynamic_slice_in_dim(vir_energy, lax.axis_index("vir") * vir_width, vir_width)
    shifted = shifted_2(integrals, "occ", 2)
    partner = lax.all_gather(shifted, "vir", axis=1, tiled=True)
    virtuals = partner.shape[1]
    pair_level = own_level + partner_level
    share_rows = virtuals // lax.axis_size("aux")
    partial_value = lax.psum_scatter(
        jnp.einsum("nbq,naq->bna", partner, integrals, preferred_element_type=jnp.float32),
        "aux",
        scatter_dimension=0,
        tiled=True,
    )
    first_row = lax.axis_index("aux") * share_rows
    vir_rows = lax.dynamic_slice_in_dim(vir_energy, first_row, share_rows)
    amplitudes = (
        partial_value
        / (pair_level[None, :, None] - vir_rows[:, None, None] - local_vir[None, None, :])
    ).astype(jnp.bfloat16)
    portion = lax.all_gather(amplitudes, "aux", axis=0, tiled=True)
    own_part = jnp.einsum("bna,nbq->naq", portion, partner, preferred_element_type=jnp.float32)
    rows_back = jnp.einsum("bna,naq->nbq", portion, integrals, preferred_element_type=jnp.float32)
    owned = lax.psum_scatter(rows_back, "vir", scatter_dimension=1, tiled=True)
    returned = shifted_2(owned, "occ", -2)
    return (own_part + returned).astype(jnp.bfloat16)


def xor_pairs(count, step):
    return [(j, j ^ step) for j in range(count)]


def aux_reduce_scatter(x):
    count = lax.axis_size("aux")
    k = lax.axis_index("aux")
    first = 0
    step = 1
    while step < count:
        half = x.shape[0] // 2
        bit = (k // step) % 2
        keep = lax.dynamic_slice_in_dim(x, bit * half, half, 0)
        send = lax.dynamic_slice_in_dim(x, (1 - bit) * half, half, 0)
        if step > 1 and NARROW_FAR:
            x = keep + lax.ppermute(send.astype(jnp.bfloat16), "aux", xor_pairs(count, step))
        else:
            x = keep + lax.ppermute(send, "aux", xor_pairs(count, step))
        first = first + bit * half
        step *= 2
    return x, first


def aux_all_gather(x):
    count = lax.axis_size("aux")
    k = lax.axis_index("aux")
    step = count // 2
    while step >= 1:
        bit = (k // step) % 2
        other = lax.ppermute(x, "aux", xor_pairs(count, step))
        x = jnp.where(bit == 0, jnp.concatenate([x, other]), jnp.concatenate([other, x]))
        step //= 2
    return x


def paired_plan(integrals, occ_energy, vir_energy):
    own = integrals[0]
    vir_rows, _ = own.shape
    cycle_size = lax.axis_size("occ")
    position = lax.axis_index("occ")
    pair_level = occ_energy[position] + occ_energy[(position - 2) % cycle_size]
    vir_pos = lax.axis_index("vir")
    vir_count = lax.axis_size("vir")
    aux_count = lax.axis_size("aux")
    share = vir_rows // aux_count
    width = vir_rows // CHUNKS

    total = None
    previous = None
    rows_done = None
    mate = None
    for t in range(CHUNKS + 1):
        parts, levels = [], []
        if t < CHUNKS:
            source = own
            if previous is not None:
                source, _ = lax.optimization_barrier((own, previous))
            piece = source[t * width:(t + 1) * width]
            arrived = shifted_2(piece, "occ", 2)
            previous = arrived
            parts.append(arrived)
            levels.append(lax.dynamic_slice_in_dim(vir_energy, vir_pos * vir_rows + t * width, width))
        if mate is not None:
            parts.append(mate)
            levels.append(
                lax.dynamic_slice_in_dim(vir_energy, (1 - vir_pos) * vir_rows + (t - 1) * width, width)
            )
        mate = shifted_2(arrived, "vir", 1) if t < CHUNKS else None
        block = jnp.concatenate(parts) if len(parts) > 1 else parts[0]
        col_level = jnp.concatenate(levels) if len(levels) > 1 else levels[0]
        partial = jnp.einsum("aq,bq->ab", own, block, preferred_element_type=jnp.float32)
        summed, first = aux_reduce_scatter(partial)
        if rows_done is not None:
            summed, _ = lax.optimization_barrier((summed, rows_done))
        row_level = lax.dynamic_slice_in_dim(vir_energy, vir_pos * vir_rows + first, share)
        amplitudes = (summed / (pair_level - row_level[:, None] - col_level[None, :])).astype(
            jnp.bfloat16
        )
        rows = aux_all_gather(amplitudes)
        rows_done = rows
        term = jnp.dot(rows, block, preferred_element_type=jnp.float32)
        total = term if total is None else total + term
    gamma_own = total
    gamma_back = total
    return (gamma_own + gamma_back).astype(jnp.bfloat16)[None]


def on_device(integrals, occ_energy, vir_energy):
    cycle_size = lax.axis_size("occ")
    pairs_here = integrals.shape[0] == 1 and 4 % cycle_size == 0 and lax.axis_size("vir") == 2
    if pairs_here and integrals.shape[1] % (CHUNKS * 8) == 0:
        return paired_plan(integrals, occ_energy, vir_energy)
    return general_plan(integrals, occ_energy, vir_energy)


def solution(mesh):
    placed = (P("occ", "vir", "aux"), P(), P())
    return jax.shard_map(
        on_device, mesh=mesh, in_specs=placed, out_specs=P("occ", "vir", "aux"), check_vma=False
    )
```

```python
import jax
import jax.numpy as jnp
from jax import lax
from jax.sharding import PartitionSpec as P

CHUNKS = 8
AUX_BY_PERMUTE = True
NARROW_FAR = False


def shifted_2(value, axis, by):
    count = lax.axis_size(axis)
    return lax.ppermute(value, axis, [(i, (i + by) % count) for i in range(count)])


def general_plan(integrals, occ_energy, vir_energy):
    row_count = integrals.shape[0]
    vir_width = integrals.shape[1]
    cycle_size = lax.axis_size("occ")
    position = lax.axis_index("occ")
    own_level = lax.dynamic_slice_in_dim(occ_energy, position * row_count, row_count)
    partner_level = lax.dynamic_slice_in_dim(
        occ_energy, (position - 2) % cycle_size * row_count, row_count
    )
    local_vir = lax.dynamic_slice_in_dim(vir_energy, lax.axis_index("vir") * vir_width, vir_width)
    shifted = shifted_2(integrals, "occ", 2)
    partner = lax.all_gather(shifted, "vir", axis=1, tiled=True)
    virtuals = partner.shape[1]
    pair_level = own_level + partner_level
    share_rows = virtuals // lax.axis_size("aux")
    partial_value = lax.psum_scatter(
        jnp.einsum("nbq,naq->bna", partner, integrals, preferred_element_type=jnp.float32),
        "aux",
        scatter_dimension=0,
        tiled=True,
    )
    first_row = lax.axis_index("aux") * share_rows
    vir_rows = lax.dynamic_slice_in_dim(vir_energy, first_row, share_rows)
    amplitudes = (
        partial_value
        / (pair_level[None, :, None] - vir_rows[:, None, None] - local_vir[None, None, :])
    ).astype(jnp.bfloat16)
    portion = lax.all_gather(amplitudes, "aux", axis=0, tiled=True)
    own_part = jnp.einsum("bna,nbq->naq", portion, partner, preferred_element_type=jnp.float32)
    rows_back = jnp.einsum("bna,naq->nbq", portion, integrals, preferred_element_type=jnp.float32)
    owned = lax.psum_scatter(rows_back, "vir", scatter_dimension=1, tiled=True)
    returned = shifted_2(owned, "occ", -2)
    return (own_part + returned).astype(jnp.bfloat16)


def xor_pairs(count, step):
    return [(j, j ^ step) for j in range(count)]


def aux_reduce_scatter(x):
    count = lax.axis_size("aux")
    k = lax.axis_index("aux")
    first = 0
    step = 1
    while step < count:
        half = x.shape[0] // 2
        bit = (k // step) % 2
        keep = lax.dynamic_slice_in_dim(x, bit * half, half, 0)
        send = lax.dynamic_slice_in_dim(x, (1 - bit) * half, half, 0)
        if step > 1 and NARROW_FAR:
            x = keep + lax.ppermute(send.astype(jnp.bfloat16), "aux", xor_pairs(count, step))
        else:
            x = keep + lax.ppermute(send, "aux", xor_pairs(count, step))
        first = first + bit * half
        step *= 2
    return x, first


def aux_all_gather(x):
    count = lax.axis_size("aux")
    k = lax.axis_index("aux")
    step = count // 2
    while step >= 1:
        bit = (k // step) % 2
        other = lax.ppermute(x, "aux", xor_pairs(count, step))
        x = jnp.where(bit == 0, jnp.concatenate([x, other]), jnp.concatenate([other, x]))
        step //= 2
    return x


def paired_plan(integrals, occ_energy, vir_energy):
    own = integrals[0]
    vir_rows, _ = own.shape
    cycle_size = lax.axis_size("occ")
    position = lax.axis_index("occ")
    pair_level = occ_energy[position] + occ_energy[(position - 2) % cycle_size]
    vir_pos = lax.axis_index("vir")
    vir_count = lax.axis_size("vir")
    aux_count = lax.axis_size("aux")
    share = vir_rows // aux_count
    width = vir_rows // CHUNKS

    total = None
    previous = None
    rows_done = None
    mate = None
    for t in range(CHUNKS + 1):
        parts, levels = [], []
        if t < CHUNKS:
            piece = own[t * width:(t + 1) * width]
            if previous is not None:
                piece, _ = lax.optimization_barrier((piece, previous))
            arrived = shifted_2(piece, "occ", 2)
            previous = arrived
            parts.append(arrived)
            levels.append(lax.dynamic_slice_in_dim(vir_energy, vir_pos * vir_rows + t * width, width))
        if mate is not None:
            parts.append(mate)
            levels.append(
                lax.dynamic_slice_in_dim(vir_energy, (1 - vir_pos) * vir_rows + (t - 1) * width, width)
            )
        mate = shifted_2(arrived, "vir", 1) if t < CHUNKS else None
        block = jnp.concatenate(parts) if len(parts) > 1 else parts[0]
        col_level = jnp.concatenate(levels) if len(levels) > 1 else levels[0]
        partial = jnp.einsum("aq,bq->ab", own, block, preferred_element_type=jnp.float32)
        summed, first = aux_reduce_scatter(partial)
        if rows_done is not None:
            summed, _ = lax.optimization_barrier((summed, rows_done))
        row_level = lax.dynamic_slice_in_dim(vir_energy, vir_pos * vir_rows + first, share)
        amplitudes = (summed / (pair_level - row_level[:, None] - col_level[None, :])).astype(
            jnp.bfloat16
        )
        rows = aux_all_gather(amplitudes)
        rows_done = rows
        term = jnp.dot(rows, block, preferred_element_type=jnp.float32)
        total = term if total is None else total + term
    gamma_own = total
    gamma_back = total
    return (gamma_own + gamma_back).astype(jnp.bfloat16)[None]


def on_device(integrals, occ_energy, vir_energy):
    cycle_size = lax.axis_size("occ")
    pairs_here = integrals.shape[0] == 1 and 4 % cycle_size == 0 and lax.axis_size("vir") == 2
    if pairs_here and integrals.shape[1] % (CHUNKS * 8) == 0:
        return paired_plan(integrals, occ_energy, vir_energy)
    return general_plan(integrals, occ_energy, vir_energy)


def solution(mesh):
    placed = (P("occ", "vir", "aux"), P(), P())
    return jax.shard_map(
        on_device, mesh=mesh, in_specs=placed, out_specs=P("occ", "vir", "aux"), check_vma=False
    )
```

```python
import jax
import jax.numpy as jnp
from jax import lax
from jax.sharding import PartitionSpec as P

WIDTHS = (128, 256, 256, 256, 128)
AUX_BY_PERMUTE = True
NARROW_FAR = False


def shifted_2(value, axis, by):
    count = lax.axis_size(axis)
    return lax.ppermute(value, axis, [(i, (i + by) % count) for i in range(count)])


def general_plan(integrals, occ_energy, vir_energy):
    row_count = integrals.shape[0]
    vir_width = integrals.shape[1]
    cycle_size = lax.axis_size("occ")
    position = lax.axis_index("occ")
    own_level = lax.dynamic_slice_in_dim(occ_energy, position * row_count, row_count)
    partner_level = lax.dynamic_slice_in_dim(
        occ_energy, (position - 2) % cycle_size * row_count, row_count
    )
    local_vir = lax.dynamic_slice_in_dim(vir_energy, lax.axis_index("vir") * vir_width, vir_width)
    shifted = shifted_2(integrals, "occ", 2)
    partner = lax.all_gather(shifted, "vir", axis=1, tiled=True)
    virtuals = partner.shape[1]
    pair_level = own_level + partner_level
    share_rows = virtuals // lax.axis_size("aux")
    partial_value = lax.psum_scatter(
        jnp.einsum("nbq,naq->bna", partner, integrals, preferred_element_type=jnp.float32),
        "aux",
        scatter_dimension=0,
        tiled=True,
    )
    first_row = lax.axis_index("aux") * share_rows
    vir_rows = lax.dynamic_slice_in_dim(vir_energy, first_row, share_rows)
    amplitudes = (
        partial_value
        / (pair_level[None, :, None] - vir_rows[:, None, None] - local_vir[None, None, :])
    ).astype(jnp.bfloat16)
    portion = lax.all_gather(amplitudes, "aux", axis=0, tiled=True)
    own_part = jnp.einsum("bna,nbq->naq", portion, partner, preferred_element_type=jnp.float32)
    rows_back = jnp.einsum("bna,naq->nbq", portion, integrals, preferred_element_type=jnp.float32)
    owned = lax.psum_scatter(rows_back, "vir", scatter_dimension=1, tiled=True)
    returned = shifted_2(owned, "occ", -2)
    return (own_part + returned).astype(jnp.bfloat16)


def xor_pairs(count, step):
    return [(j, j ^ step) for j in range(count)]


def aux_reduce_scatter(x):
    count = lax.axis_size("aux")
    k = lax.axis_index("aux")
    first = 0
    step = 1
    while step < count:
        half = x.shape[0] // 2
        bit = (k // step) % 2
        keep = lax.dynamic_slice_in_dim(x, bit * half, half, 0)
        send = lax.dynamic_slice_in_dim(x, (1 - bit) * half, half, 0)
        if step > 1 and NARROW_FAR:
            x = keep + lax.ppermute(send.astype(jnp.bfloat16), "aux", xor_pairs(count, step))
        else:
            x = keep + lax.ppermute(send, "aux", xor_pairs(count, step))
        first = first + bit * half
        step *= 2
    return x, first


def aux_all_gather(x):
    count = lax.axis_size("aux")
    k = lax.axis_index("aux")
    step = count // 2
    while step >= 1:
        bit = (k // step) % 2
        other = lax.ppermute(x, "aux", xor_pairs(count, step))
        x = jnp.where(bit == 0, jnp.concatenate([x, other]), jnp.concatenate([other, x]))
        step //= 2
    return x


def paired_plan(integrals, occ_energy, vir_energy):
    own = integrals[0]
    vir_rows, _ = own.shape
    cycle_size = lax.axis_size("occ")
    position = lax.axis_index("occ")
    pair_level = occ_energy[position] + occ_energy[(position - 2) % cycle_size]
    vir_pos = lax.axis_index("vir")
    vir_count = lax.axis_size("vir")
    aux_count = lax.axis_size("aux")
    share = vir_rows // aux_count
    widths = [w * (vir_rows // sum(WIDTHS)) for w in WIDTHS]
    starts = [sum(widths[:c]) for c in range(len(widths))]

    total = None
    previous = None
    rows_done = None
    mate = None
    for t in range(len(widths) + 1):
        parts, levels = [], []
        if t < len(widths):
            piece = own[starts[t]:starts[t] + widths[t]]
            if previous is not None:
                piece, _ = lax.optimization_barrier((piece, previous))
            arrived = shifted_2(piece, "occ", 2)
            previous = arrived
            parts.append(arrived)
            levels.append(
                lax.dynamic_slice_in_dim(vir_energy, vir_pos * vir_rows + starts[t], widths[t])
            )
        if mate is not None:
            parts.append(mate)
            levels.append(
                lax.dynamic_slice_in_dim(
                    vir_energy, (1 - vir_pos) * vir_rows + starts[t - 1], widths[t - 1]
                )
            )
        mate = shifted_2(arrived, "vir", 1) if t < len(widths) else None
        block = jnp.concatenate(parts) if len(parts) > 1 else parts[0]
        col_level = jnp.concatenate(levels) if len(levels) > 1 else levels[0]
        partial = jnp.einsum("aq,bq->ab", own, block, preferred_element_type=jnp.float32)
        summed, first = aux_reduce_scatter(partial)
        if rows_done is not None:
            summed, _ = lax.optimization_barrier((summed, rows_done))
        row_level = lax.dynamic_slice_in_dim(vir_energy, vir_pos * vir_rows + first, share)
        amplitudes = (summed / (pair_level - row_level[:, None] - col_level[None, :])).astype(
            jnp.bfloat16
        )
        rows = aux_all_gather(amplitudes)
        rows_done = rows
        term = jnp.dot(rows, block, preferred_element_type=jnp.float32)
        total = term if total is None else total + term
    gamma_own = total
    gamma_back = total
    return (gamma_own + gamma_back).astype(jnp.bfloat16)[None]


def on_device(integrals, occ_energy, vir_energy):
    cycle_size = lax.axis_size("occ")
    pairs_here = integrals.shape[0] == 1 and 4 % cycle_size == 0 and lax.axis_size("vir") == 2
    if pairs_here and integrals.shape[1] % sum(WIDTHS) == 0:
        return paired_plan(integrals, occ_energy, vir_energy)
    return general_plan(integrals, occ_energy, vir_energy)


def solution(mesh):
    placed = (P("occ", "vir", "aux"), P(), P())
    return jax.shard_map(
        on_device, mesh=mesh, in_specs=placed, out_specs=P("occ", "vir", "aux"), check_vma=False
    )
```

```python
import jax
import jax.numpy as jnp
from jax import lax
from jax.sharding import PartitionSpec as P

CHUNKS = 4
AUX_BY_PERMUTE = True
NARROW_FAR = False


def shifted_2(value, axis, by):
    count = lax.axis_size(axis)
    return lax.ppermute(value, axis, [(i, (i + by) % count) for i in range(count)])


def general_plan(integrals, occ_energy, vir_energy):
    row_count = integrals.shape[0]
    vir_width = integrals.shape[1]
    cycle_size = lax.axis_size("occ")
    position = lax.axis_index("occ")
    own_level = lax.dynamic_slice_in_dim(occ_energy, position * row_count, row_count)
    partner_level = lax.dynamic_slice_in_dim(
        occ_energy, (position - 2) % cycle_size * row_count, row_count
    )
    local_vir = lax.dynamic_slice_in_dim(vir_energy, lax.axis_index("vir") * vir_width, vir_width)
    shifted = shifted_2(integrals, "occ", 2)
    partner = lax.all_gather(shifted, "vir", axis=1, tiled=True)
    virtuals = partner.shape[1]
    pair_level = own_level + partner_level
    share_rows = virtuals // lax.axis_size("aux")
    partial_value = lax.psum_scatter(
        jnp.einsum("nbq,naq->bna", partner, integrals, preferred_element_type=jnp.float32),
        "aux",
        scatter_dimension=0,
        tiled=True,
    )
    first_row = lax.axis_index("aux") * share_rows
    vir_rows = lax.dynamic_slice_in_dim(vir_energy, first_row, share_rows)
    amplitudes = (
        partial_value
        / (pair_level[None, :, None] - vir_rows[:, None, None] - local_vir[None, None, :])
    ).astype(jnp.bfloat16)
    portion = lax.all_gather(amplitudes, "aux", axis=0, tiled=True)
    own_part = jnp.einsum("bna,nbq->naq", portion, partner, preferred_element_type=jnp.float32)
    rows_back = jnp.einsum("bna,naq->nbq", portion, integrals, preferred_element_type=jnp.float32)
    owned = lax.psum_scatter(rows_back, "vir", scatter_dimension=1, tiled=True)
    returned = shifted_2(owned, "occ", -2)
    return (own_part + returned).astype(jnp.bfloat16)


def xor_pairs(count, step):
    return [(j, j ^ step) for j in range(count)]


def aux_reduce_scatter(x):
    count = lax.axis_size("aux")
    k = lax.axis_index("aux")
    first = 0
    step = 1
    while step < count:
        half = x.shape[0] // 2
        bit = (k // step) % 2
        keep = lax.dynamic_slice_in_dim(x, bit * half, half, 0)
        send = lax.dynamic_slice_in_dim(x, (1 - bit) * half, half, 0)
        if step > 1 and NARROW_FAR:
            x = keep + lax.ppermute(send.astype(jnp.bfloat16), "aux", xor_pairs(count, step))
        else:
            x = keep + lax.ppermute(send, "aux", xor_pairs(count, step))
        first = first + bit * half
        step *= 2
    return x, first


def aux_all_gather(x):
    count = lax.axis_size("aux")
    k = lax.axis_index("aux")
    step = count // 2
    while step >= 1:
        bit = (k // step) % 2
        other = lax.ppermute(x, "aux", xor_pairs(count, step))
        x = jnp.where(bit == 0, jnp.concatenate([x, other]), jnp.concatenate([other, x]))
        step //= 2
    return x


def paired_plan(integrals, occ_energy, vir_energy):
    own = integrals[0]
    vir_rows, _ = own.shape
    cycle_size = lax.axis_size("occ")
    position = lax.axis_index("occ")
    pair_level = occ_energy[position] + occ_energy[(position - 2) % cycle_size]
    vir_pos = lax.axis_index("vir")
    vir_count = lax.axis_size("vir")
    aux_count = lax.axis_size("aux")
    share = vir_rows // aux_count
    width = vir_rows // CHUNKS

    total = None
    previous = None
    rows_done = None
    mate = None
    for t in range(CHUNKS + 1):
        parts, levels = [], []
        if t < CHUNKS:
            piece = own[t * width:(t + 1) * width]
            if previous is not None:
                piece, _ = lax.optimization_barrier((piece, previous))
            arrived = shifted_2(piece, "occ", 2)
            previous = arrived
            parts.append(arrived)
            levels.append(lax.dynamic_slice_in_dim(vir_energy, vir_pos * vir_rows + t * width, width))
        if mate is not None:
            parts.append(mate)
            levels.append(
                lax.dynamic_slice_in_dim(vir_energy, (1 - vir_pos) * vir_rows + (t - 1) * width, width)
            )
        mate = shifted_2(arrived, "vir", 1) if t < CHUNKS else None
        block = jnp.concatenate(parts) if len(parts) > 1 else parts[0]
        col_level = jnp.concatenate(levels) if len(levels) > 1 else levels[0]
        partial = jnp.einsum("aq,bq->ab", own, block, preferred_element_type=jnp.float32)
        summed, first = aux_reduce_scatter(partial)
        if rows_done is not None:
            summed, _ = lax.optimization_barrier((summed, rows_done))
        row_level = lax.dynamic_slice_in_dim(vir_energy, vir_pos * vir_rows + first, share)
        amplitudes = (summed / (pair_level - row_level[:, None] - col_level[None, :])).astype(
            jnp.bfloat16
        )
        rows = aux_all_gather(amplitudes)
        rows_done = amplitudes
        term = jnp.dot(rows, block, preferred_element_type=jnp.float32)
        total = term if total is None else total + term
    gamma_own = total
    gamma_back = total
    return (gamma_own + gamma_back).astype(jnp.bfloat16)[None]


def on_device(integrals, occ_energy, vir_energy):
    cycle_size = lax.axis_size("occ")
    pairs_here = integrals.shape[0] == 1 and 4 % cycle_size == 0 and lax.axis_size("vir") == 2
    if pairs_here and integrals.shape[1] % (CHUNKS * 8) == 0:
        return paired_plan(integrals, occ_energy, vir_energy)
    return general_plan(integrals, occ_energy, vir_energy)


def solution(mesh):
    placed = (P("occ", "vir", "aux"), P(), P())
    return jax.shard_map(
        on_device, mesh=mesh, in_specs=placed, out_specs=P("occ", "vir", "aux"), check_vma=False
    )
```

```python
import jax
import jax.numpy as jnp
from jax import lax
from jax.sharding import PartitionSpec as P

CHUNKS = 2
AUX_BY_PERMUTE = True
NARROW_FAR = False


def shifted_2(value, axis, by):
    count = lax.axis_size(axis)
    return lax.ppermute(value, axis, [(i, (i + by) % count) for i in range(count)])


def general_plan(integrals, occ_energy, vir_energy):
    row_count = integrals.shape[0]
    vir_width = integrals.shape[1]
    cycle_size = lax.axis_size("occ")
    position = lax.axis_index("occ")
    own_level = lax.dynamic_slice_in_dim(occ_energy, position * row_count, row_count)
    partner_level = lax.dynamic_slice_in_dim(
        occ_energy, (position - 2) % cycle_size * row_count, row_count
    )
    local_vir = lax.dynamic_slice_in_dim(vir_energy, lax.axis_index("vir") * vir_width, vir_width)
    shifted = shifted_2(integrals, "occ", 2)
    partner = lax.all_gather(shifted, "vir", axis=1, tiled=True)
    virtuals = partner.shape[1]
    pair_level = own_level + partner_level
    share_rows = virtuals // lax.axis_size("aux")
    partial_value = lax.psum_scatter(
        jnp.einsum("nbq,naq->bna", partner, integrals, preferred_element_type=jnp.float32),
        "aux",
        scatter_dimension=0,
        tiled=True,
    )
    first_row = lax.axis_index("aux") * share_rows
    vir_rows = lax.dynamic_slice_in_dim(vir_energy, first_row, share_rows)
    amplitudes = (
        partial_value
        / (pair_level[None, :, None] - vir_rows[:, None, None] - local_vir[None, None, :])
    ).astype(jnp.bfloat16)
    portion = lax.all_gather(amplitudes, "aux", axis=0, tiled=True)
    own_part = jnp.einsum("bna,nbq->naq", portion, partner, preferred_element_type=jnp.float32)
    rows_back = jnp.einsum("bna,naq->nbq", portion, integrals, preferred_element_type=jnp.float32)
    owned = lax.psum_scatter(rows_back, "vir", scatter_dimension=1, tiled=True)
    returned = shifted_2(owned, "occ", -2)
    return (own_part + returned).astype(jnp.bfloat16)


def xor_pairs(count, step):
    return [(j, j ^ step) for j in range(count)]


def aux_reduce_scatter(x):
    count = lax.axis_size("aux")
    k = lax.axis_index("aux")
    first = 0
    step = 1
    while step < count:
        half = x.shape[0] // 2
        bit = (k // step) % 2
        keep = lax.dynamic_slice_in_dim(x, bit * half, half, 0)
        send = lax.dynamic_slice_in_dim(x, (1 - bit) * half, half, 0)
        if step > 1 and NARROW_FAR:
            x = keep + lax.ppermute(send.astype(jnp.bfloat16), "aux", xor_pairs(count, step))
        else:
            x = keep + lax.ppermute(send, "aux", xor_pairs(count, step))
        first = first + bit * half
        step *= 2
    return x, first


def aux_all_gather(x):
    count = lax.axis_size("aux")
    k = lax.axis_index("aux")
    step = count // 2
    while step >= 1:
        bit = (k // step) % 2
        other = lax.ppermute(x, "aux", xor_pairs(count, step))
        x = jnp.where(bit == 0, jnp.concatenate([x, other]), jnp.concatenate([other, x]))
        step //= 2
    return x


def paired_plan(integrals, occ_energy, vir_energy):
    own = integrals[0]
    vir_rows, _ = own.shape
    cycle_size = lax.axis_size("occ")
    position = lax.axis_index("occ")
    pair_level = occ_energy[position] + occ_energy[(position - 2) % cycle_size]
    vir_pos = lax.axis_index("vir")
    vir_count = lax.axis_size("vir")
    aux_count = lax.axis_size("aux")
    share = vir_rows // aux_count
    width = vir_rows // CHUNKS

    total = None
    previous = None
    rows_done = None
    mate = None
    for t in range(CHUNKS + 1):
        parts, levels = [], []
        if t < CHUNKS:
            piece = own[t * width:(t + 1) * width]
            if previous is not None:
                piece, _ = lax.optimization_barrier((piece, previous))
            arrived = shifted_2(piece, "occ", 2)
            previous = arrived
            parts.append(arrived)
            levels.append(lax.dynamic_slice_in_dim(vir_energy, vir_pos * vir_rows + t * width, width))
        if mate is not None:
            parts.append(mate)
            levels.append(
                lax.dynamic_slice_in_dim(vir_energy, (1 - vir_pos) * vir_rows + (t - 1) * width, width)
            )
        mate = shifted_2(arrived, "vir", 1) if t < CHUNKS else None
        block = jnp.concatenate(parts) if len(parts) > 1 else parts[0]
        col_level = jnp.concatenate(levels) if len(levels) > 1 else levels[0]
        partial = jnp.einsum("aq,bq->ab", own, block, preferred_element_type=jnp.float32)
        summed, first = aux_reduce_scatter(partial)
        if rows_done is not None:
            summed, _ = lax.optimization_barrier((summed, rows_done))
        row_level = lax.dynamic_slice_in_dim(vir_energy, vir_pos * vir_rows + first, share)
        amplitudes = (summed / (pair_level - row_level[:, None] - col_level[None, :])).astype(
            jnp.bfloat16
        )
        rows = aux_all_gather(amplitudes)
        rows_done = rows
        term = jnp.dot(rows, block, preferred_element_type=jnp.float32)
        total = term if total is None else total + term
    gamma_own = total
    gamma_back = total
    return (gamma_own + gamma_back).astype(jnp.bfloat16)[None]


def on_device(integrals, occ_energy, vir_energy):
    cycle_size = lax.axis_size("occ")
    pairs_here = integrals.shape[0] == 1 and 4 % cycle_size == 0 and lax.axis_size("vir") == 2
    if pairs_here and integrals.shape[1] % (CHUNKS * 8) == 0:
        return paired_plan(integrals, occ_energy, vir_energy)
    return general_plan(integrals, occ_energy, vir_energy)


def solution(mesh):
    placed = (P("occ", "vir", "aux"), P(), P())
    return jax.shard_map(
        on_device, mesh=mesh, in_specs=placed, out_specs=P("occ", "vir", "aux"), check_vma=False
    )
```
